32 devices in a mesh: dp: 8 (over z, y), tensor: 4 (over x, core).
Axes of the slice: x: 2, y: 2, z: 4, core: 2. Of those that a mesh axis runs over, the one named last changes fastest.
Arguments:
- query: bfloat16 [384, 8192], P('dp', 'tensor'), may hold values from -128 to 128
- new_key: bfloat16 [384, 512], P('dp', 'tensor'), may hold values from -6 to 6
- new_value: bfloat16 [384, 512], P('dp', 'tensor'), may hold values from -6 to 6
- cache_key: bfloat16 [384, 128, 512], P('dp', None, 'tensor'), may hold values from -6 to 6
- cache_value: bfloat16 [384, 128, 512], P('dp', None, 'tensor'), may hold values from -6 to 6
- lengths: int32 [384], P('dp'), may hold values from 1 to 128, as said below
- hidden_in: bfloat16 [384, 4096], P(('dp', 'tensor')), may hold values from -60 to 60
- out_weight: bfloat16 [8192, 4096], P('tensor', 'dp'), may hold values from -0.0625 to 0.0625
- norm_gain: float32 [4096], replicated, may hold values from 0.25 to 1.75
- route_ids: int32 [384, 8], P(('dp', 'tensor')), may hold values from 0 to 31, all different within a row; in each aligned block of 12 rows (0 to 11, 12 to 23, ...) at most 9 rows name the same one
- route_weight: float32 [384, 8], P(('dp', 'tensor')), may hold values from 0.03 to 0.3
- w_gate: bfloat16 [32, 4096, 768], P(('dp', 'tensor')), may hold values from -0.09375 to 0.09375
- w_up: bfloat16 [32, 4096, 768], P(('dp', 'tensor')), may hold values from -0.09375 to 0.09375
- w_down: bfloat16 [32, 768, 4096], P(('dp', 'tensor')), may hold values from -0.21875 to 0.21875
Outputs:
- attended: bfloat16 [384, 4096], P(('dp', 'tensor'))
- expert_mix: bfloat16 [384, 4096], P(('dp', 'tensor'))
The draws below stay inside these ranges and needn't reach their ends.
Inputs may be any that keep to these rules, and one draw needn't show every extreme that they name: `lengths`: row 0 holds 128 positions. `route_ids`: A row names 8 different experts. In each aligned block of 12 rows (the rows of one device along dp+tensor) no expert is named by more than 9 rows, a bound that some block reaches.
All inputs are finite; a program needn't handle non-finite values.
Results may differ from the reference program's by a relative error of at most 0.013.
Values may be sent and summed in bfloat16 or wider, within the bound.
No kernel may reach another device: no remote copies, remote signals or barrier semaphores. Data moves between devices by JAX's collectives and lax.ppermute only.
A program may use at most 128 MiB of HBM per device.

```python
import math
import jax
import jax.numpy as jnp
import numpy as np
from jax import lax

D = 4096
H = 64
KV = 4
HD = 128
FFW = 768
TOP = 8
ROWS_DEV = 48
CACHE = 128
EXPERTS = 32
ROWS = 384
T_DEV = 12
CAP = 9


def draw_query(key, part):
    result = jnp.clip(jax.random.normal(jax.random.fold_in(key, 1), (ROWS, H * HD), jnp.float32), -6.0, 6.0)
    return result.astype(jnp.bfloat16)


def draw_cache_key(key, part):
    result = jnp.clip(jax.random.normal(jax.random.fold_in(key, 2), (ROWS, CACHE, KV * HD), jnp.float32), -6.0, 6.0)
    return result.astype(jnp.bfloat16)


def draw_hidden_in(key, part):
    low = math.log(0.3)
    high = math.log(3.0)
    row_scale = jnp.exp(jax.random.uniform(jax.random.fold_in(key, 21), (ROWS, 1), jnp.float32, low, high))
    column_scale = jnp.exp(jax.random.uniform(jax.random.fold_in(key, 22), (1, D), jnp.float32, low, high))
    core = jnp.clip(jax.random.normal(jax.random.fold_in(key, 23), (ROWS, D), jnp.float32), -6.0, 6.0)
    return (core * row_scale * column_scale).astype(jnp.bfloat16)


def draw_lengths(key, part):
    block_most = jax.random.randint(jax.random.fold_in(key, 31), (ROWS // ROWS_DEV, 1), 1, CACHE + 1)
    raw_draw = jax.random.randint(jax.random.fold_in(key, 32), (ROWS // ROWS_DEV, ROWS_DEV), 0, CACHE)
    filled = (1 + raw_draw % block_most).reshape(ROWS).astype(jnp.int32)
    return filled.at[0].set(CACHE)


def block_scale(rng, extent, cuts, least, largest):
    def one(dim, blocks):
        draws = jax.random.uniform(jax.random.fold_in(jax.random.fold_in(rng, 6), dim), (blocks,), jnp.float32, least / len(cuts), largest / len(cuts))
        return jnp.repeat(jnp.exp(draws), extent[dim] // blocks).reshape((-1,) + (1,) * (len(extent) - dim - 1))

    loudness = one(*cuts[0])
    for cut in cuts[1:]:
        loudness = loudness * one(*cut)
    return loudness


def assign_block(key, own, number, rows, count, top, most, slope):
    ranking = jax.random.permutation(key, count)
    crowded, ordinary = load_shares(count, rows * top, most, slope, True), load_shares(count, rows * top, most, slope, False)
    places = jnp.arange(count)

    def named(tallies, turn):
        used = int((tallies > 0).sum())
        fixed = max(1, used // 4)
        moved = fixed + (places - fixed + turn * (used - fixed)) % max(1, count - fixed)
        return jnp.zeros((count,), jnp.int32).at[ranking[jnp.where(places < fixed, places, moved)]].set(jnp.asarray(tallies, jnp.int32))

    tallies = jnp.where(number % 4 == 0, named(crowded, number // 4), named(ordinary, number - number // 4 - 1))
    mixed = jax.random.permutation(jax.random.fold_in(own, 3), count)
    source_of, taker = mixed[0:count // 2 * 2:2], mixed[1:count // 2 * 2:2]
    slack = jnp.minimum(tallies[source_of] - 1, most - tallies[taker]) // 2
    slack = jnp.where((source_of == ranking[0]) | (taker == ranking[0]) | (tallies[taker] == 0), 0, jnp.maximum(slack, 0))
    moved = jax.random.randint(jax.random.fold_in(own, 4), (count // 2,), 0, 1 << 20) % (slack + 1)
    tallies = tallies.at[source_of].add(-moved).at[taker].add(moved)
    labels = jnp.searchsorted(jnp.cumsum(tallies), jnp.arange(rows * top), side="right").astype(jnp.int32)
    table = labels.reshape(top, rows).T
    table = table[jax.random.permutation(jax.random.fold_in(own, 1), rows)]
    turn = jax.random.randint(jax.random.fold_in(own, 2), (rows, 1), 0, top)
    return jnp.take_along_axis(table, (jnp.arange(top)[None, :] + turn) % top, axis=1)


def load_shares(amount, total, limit, slope, full):
    portions = [(1 << 20) // math.isqrt(standing ** slope) + 1 for standing in range(1, amount + 1)]
    largest = limit if full else min(limit, max(-(-total // amount), total * portions[0] // sum(portions)))
    least = 1 if total - largest >= amount - 1 else 0
    counts, surplus = [largest] + [least] * (amount - 1), total - largest - least * (amount - 1)
    while surplus > 0:
        free = [i for i in range(1, amount) if counts[i] < largest] or [i for i in range(1, amount) if counts[i] < limit]
        mass, left = sum([portions[i] for i in free]), surplus
        for i in free:
            extra = min(limit - counts[i], max(1, left * portions[i] // mass), surplus)
            counts[i] = counts[i] + extra
            surplus = surplus - extra
    return np.array(counts)


def normal_values(stream_key, shape, width, most, shards=(), kind=jnp.bfloat16):
    values = jax.random.normal(stream_key, shape, jnp.float32) * width
    if len(shards) > 0:
        values = block_scale(stream_key, shape, shards, -0.22, 0.18) * values
    return jnp.clip(values, min=-most, max=most).astype(kind)


def setup_inputs(seed: int = 0) -> dict:
    arg_keys = jax.random.split(jax.random.key(seed), 15)
    query = draw_query(jax.random.fold_in(arg_keys[14], 71), 0)
    new_key = normal_values(arg_keys[1], (ROWS, KV * HD), 1.0, 6.0, ((0, 8), (1, 4)))
    new_value = normal_values(arg_keys[2], (ROWS, KV * HD), 1.0, 6.0, ((0, 8), (1, 4)))
    cache_key = draw_cache_key(jax.random.fold_in(arg_keys[14], 71), 0)
    cache_value = normal_values(arg_keys[4], (ROWS, CACHE, KV * HD), 1.0, 6.0, ((0, 8), (2, 4)))
    lengths = draw_lengths(jax.random.fold_in(arg_keys[14], 71), 0)
    hidden_in = draw_hidden_in(jax.random.fold_in(arg_keys[14], 71), 0)
    out_weight = normal_values(arg_keys[7], (H * HD, D), (H * HD) ** -0.5, 0.0625, ((0, 4), (1, 8)))
    norm_gain = jnp.clip(1.0 + 0.15 * jax.random.normal(arg_keys[8], (D,), jnp.float32), 0.25, 1.75)
    route_ids_keys = jax.random.split(jax.random.fold_in(arg_keys[9], 1), ROWS // T_DEV)
    route_ids_turns = jax.random.permutation(jax.random.fold_in(arg_keys[9], 3), ROWS // T_DEV)
    route_ids = jax.vmap(lambda own, number: assign_block(jax.random.fold_in(arg_keys[9], 2), own, number, T_DEV, EXPERTS, TOP, CAP, 2))(route_ids_keys, route_ids_turns).reshape((ROWS, TOP))
    route_weight = jnp.clip(jnp.exp(math.log(0.3) - 2.3025852 * jax.random.uniform(arg_keys[10], (ROWS, TOP), jnp.float32) ** block_scale(arg_keys[10], (ROWS, TOP), ((0, 32),), -0.2, 0.2)), 0.03, 0.3)
    w_gate = normal_values(arg_keys[11], (EXPERTS, D, FFW), D ** -0.5, 0.09375, ((0, 32),))
    w_up = normal_values(arg_keys[12], (EXPERTS, D, FFW), D ** -0.5, 0.09375, ((0, 32),))
    w_down = normal_values(arg_keys[13], (EXPERTS, FFW, D), FFW ** -0.5, 0.21875, ((0, 32),))
    return {"query": query, "new_key": new_key, "new_value": new_value, "cache_key": cache_key, "cache_value": cache_value, "lengths": lengths, "hidden_in": hidden_in, "out_weight": out_weight, "norm_gain": norm_gain, "route_ids": route_ids, "route_weight": route_weight, "w_gate": w_gate, "w_up": w_up, "w_down": w_down}


def attend(query, new_key, new_value, cache_key, cache_value, lengths):
    row_count = query.shape[0]
    cache_len = cache_key.shape[1]
    grouping = H // KV
    queries = query.astype(jnp.float32).reshape(row_count, KV, grouping, HD)
    cache_keys = cache_key.astype(jnp.float32).reshape(row_count, cache_len, KV, HD)
    values = cache_value.astype(jnp.float32).reshape(row_count, cache_len, KV, HD)
    own_key = new_key.astype(jnp.float32).reshape(row_count, KV, HD)
    own_value = new_value.astype(jnp.float32).reshape(row_count, KV, HD)
    factor = 1.0 / math.sqrt(HD)
    scores = jnp.einsum('rkgd,rckd->rkgc', queries, cache_keys) * factor
    own_score = jnp.einsum('rkgd,rkd->rkg', queries, own_key) * factor
    visible = (jnp.arange(cache_len, dtype=jnp.int32)[None, :] < lengths[:, None])[:, None, None, :]
    highest = jnp.maximum(lax.optimization_barrier(jnp.max(jnp.where(visible, scores, -1e+30), axis=-1)), own_score)
    exponent = jnp.where(visible, jnp.exp(scores - highest[..., None]), 0.0)
    own_exponent = jnp.exp(own_score - highest)
    totals = lax.optimization_barrier(jnp.sum(exponent, axis=-1)) + own_exponent
    probability = (exponent / totals[..., None]).astype(jnp.bfloat16)
    own_probability = (own_exponent / totals).astype(jnp.bfloat16)
    combined = jnp.einsum('rkgc,rckd->rkgd', probability.astype(jnp.float32), values)
    combined = combined + own_probability.astype(jnp.float32)[..., None] * own_value[:, :, None, :]
    return combined.reshape(row_count, H * HD).astype(jnp.bfloat16)

def reference(query, new_key, new_value, cache_key, cache_value, lengths, hidden_in, out_weight, norm_gain, route_ids, route_weight, w_gate, w_up, w_down):
    heads_out = attend(query, new_key, new_value, cache_key, cache_value, lengths)
    projected = jnp.dot(heads_out, out_weight, preferred_element_type=jnp.float32)
    attended = (hidden_in.astype(jnp.float32) + projected).astype(jnp.bfloat16)
    widened = attended.astype(jnp.float32)
    scaled = widened * lax.rsqrt(lax.optimization_barrier(jnp.mean(widened * widened, axis=-1, keepdims=True)) + 1e-06)
    normed = (scaled * norm_gain).astype(jnp.bfloat16)
    pair_count = ROWS * TOP
    flat_ids = route_ids.reshape(pair_count)
    inbound = CAP * EXPERTS

    def add_expert(expert, returned):
        picked = jnp.nonzero(flat_ids == expert, size=inbound, fill_value=pair_count)[0].astype(jnp.int32)
        token_rows = normed[jnp.minimum(picked, pair_count - 1) // TOP]
        gate_part = jnp.dot(token_rows, w_gate[expert], preferred_element_type=jnp.float32)
        up_part = jnp.dot(token_rows, w_up[expert], preferred_element_type=jnp.float32)
        activation = (jax.nn.silu(gate_part) * up_part).astype(jnp.bfloat16)
        outputs = jnp.dot(activation, w_down[expert], preferred_element_type=jnp.float32).astype(jnp.bfloat16)
        return returned.at[picked].set(outputs, mode='drop')
    returned = lax.fori_loop(0, EXPERTS, add_expert, jnp.zeros((pair_count, D), jnp.bfloat16))
    weighted = route_weight[..., None] * returned.reshape(ROWS, TOP, D).astype(jnp.float32)
    expert_mix = lax.optimization_barrier(jnp.sum(weighted, axis=1)).astype(jnp.bfloat16)
    return (attended, expert_mix)
```

```python
import math

import jax
import jax.numpy as jnp
import numpy as np
from jax import lax
from jax.sharding import Mesh
from jax.sharding import PartitionSpec as P

HD = 128
DP = ("zh", "dl")
HALF = ("dl", "tensor")


def attend_local(query, new_key, new_value, cache_key, cache_value, lengths):
    row_count = query.shape[0]
    cache_len = cache_key.shape[1]
    kv_here = new_key.shape[1] // HD
    grouping = query.shape[1] // (kv_here * HD)
    queries = query.reshape(row_count, kv_here, grouping, HD)
    cache_keys = cache_key.reshape(row_count, cache_len, kv_here, HD)
    values = cache_value.reshape(row_count, cache_len, kv_here, HD)
    own_key = new_key.reshape(row_count, kv_here, HD)
    own_value = new_value.reshape(row_count, kv_here, HD)
    factor = 1.0 / math.sqrt(HD)
    scores = (
        jnp.einsum("rkgd,rckd->rkgc", queries, cache_keys, preferred_element_type=jnp.float32)
        * factor
    )
    own_score = (
        jnp.einsum("rkgd,rkd->rkg", queries, own_key, preferred_element_type=jnp.float32) * factor
    )
    visible = (jnp.arange(cache_len, dtype=jnp.int32)[None, :] < lengths[:, None])[:, None, None, :]
    highest = jnp.maximum(jnp.max(jnp.where(visible, scores, -1e30), axis=-1), own_score)
    exponent = jnp.where(visible, jnp.exp(scores - highest[..., None]), 0.0)
    own_exponent = jnp.exp(own_score - highest)
    totals = jnp.sum(exponent, axis=-1) + own_exponent
    probability = (exponent / totals[..., None]).astype(jnp.bfloat16)
    own_probability = (own_exponent / totals).astype(jnp.bfloat16)
    combined = jnp.einsum(
        "rkgc,rckd->rkgd", probability, values, preferred_element_type=jnp.float32
    )
    combined = (
        combined
        + own_probability.astype(jnp.float32)[..., None]
        * own_value.astype(jnp.float32)[:, :, None, :]
    )
    return combined.reshape(row_count, kv_here * grouping * HD).astype(jnp.bfloat16)


def swap_halves(x):
    return lax.ppermute(x, "zh", [(0, 1), (1, 0)])


def expert_layer(normed, route_ids, route_weight, w_gate, w_up, w_down):
    tok_here, width = normed.shape
    chosen_count = route_ids.shape[1]
    n_half = lax.axis_size("dl") * lax.axis_size("tensor")
    experts_all = 2 * n_half
    capacity = 2 * max(2, 3 * tok_here * chosen_count // experts_all)
    side = lax.axis_index("zh")
    other_rows = swap_halves(normed)
    other_ids = swap_halves(route_ids)
    other_weight = swap_halves(route_weight)
    first = side == 0
    rows = jnp.where(first, jnp.concatenate([normed, other_rows]), jnp.concatenate([other_rows, normed]))
    ids = jnp.where(first, jnp.concatenate([route_ids, other_ids]), jnp.concatenate([other_ids, route_ids]))
    weights = jnp.where(
        first,
        jnp.concatenate([route_weight, other_weight]),
        jnp.concatenate([other_weight, route_weight]),
    )
    held = 2 * tok_here
    pair_count = held * chosen_count
    local_ids = ids.reshape(pair_count) - side * n_half
    expert_hits = (local_ids[:, None] == jnp.arange(n_half, dtype=jnp.int32)[None, :]).astype(
        jnp.int32
    )
    earlier = jnp.cumsum(expert_hits, axis=0) - expert_hits
    slot_index = jnp.sum(earlier * expert_hits, axis=1)
    in_half = jnp.sum(expert_hits, axis=1) > 0
    target = jnp.where(in_half, local_ids * capacity + slot_index, -1)
    placement = (
        jnp.arange(n_half * capacity, dtype=jnp.int32)[:, None] == target[None, :]
    ).astype(jnp.bfloat16)
    token_place = jnp.sum(placement.reshape(n_half * capacity, held, chosen_count), axis=2)
    outgoing = jnp.dot(token_place, rows, preferred_element_type=jnp.float32).astype(jnp.bfloat16)
    outgoing = outgoing.reshape(n_half, capacity, width)
    received = lax.all_to_all(outgoing, HALF, split_axis=0, concat_axis=0, tiled=True)
    flat_rows = received.reshape(-1, width)
    gate_part = jnp.dot(flat_rows, w_gate[0], preferred_element_type=jnp.float32)
    up_part = jnp.dot(flat_rows, w_up[0], preferred_element_type=jnp.float32)
    activation = (jax.nn.silu(gate_part) * up_part).astype(jnp.bfloat16)
    result = jnp.dot(activation, w_down[0], preferred_element_type=jnp.float32).astype(jnp.bfloat16)
    returned = lax.all_to_all(
        result.reshape(received.shape), HALF, split_axis=0, concat_axis=0, tiled=True
    )
    returned = returned.reshape(n_half * capacity, width)
    pair_rows = jnp.einsum("sp,sd->pd", placement, returned, preferred_element_type=jnp.float32)
    weighted = weights[..., None] * pair_rows.reshape(held, chosen_count, width)
    partial = jnp.sum(weighted, axis=1)
    mine = jnp.where(first, partial[:tok_here], partial[tok_here:])
    theirs = jnp.where(first, partial[tok_here:], partial[:tok_here])
    return (mine + swap_halves(theirs)).astype(jnp.bfloat16)


def shards(
    query,
    new_key,
    new_value,
    cache_key,
    cache_value,
    lengths,
    hidden_in,
    out_weight,
    norm_gain,
    route_ids,
    route_weight,
    w_gate,
    w_up,
    w_down,
):
    heads_out = attend_local(query, new_key, new_value, cache_key, cache_value, lengths)
    partial_cols = jnp.dot(
        lax.all_gather(heads_out, DP, axis=0, tiled=True),
        out_weight,
        preferred_element_type=jnp.float32,
    )
    by_rows = lax.all_to_all(partial_cols, DP, split_axis=0, concat_axis=1, tiled=True)
    summed = lax.psum_scatter(by_rows, "tensor", scatter_dimension=0, tiled=True)
    attended = (hidden_in.astype(jnp.float32) + summed).astype(jnp.bfloat16)
    widened = attended.astype(jnp.float32)
    scaled = widened * lax.rsqrt(jnp.mean(widened * widened, axis=-1, keepdims=True) + 1e-06)
    normed = (scaled * norm_gain).astype(jnp.bfloat16)
    expert_mix = expert_layer(normed, route_ids, route_weight, w_gate, w_up, w_down)
    return (attended, expert_mix)


def solution(mesh):
    n_dp = mesh.shape["dp"]
    devices = np.asarray(mesh.devices).reshape(2, n_dp // 2, mesh.shape["tensor"])
    split_mesh = Mesh(devices, ("zh", "dl", "tensor"))
    rows = DP + ("tensor",)
    in_specs = (
        P(DP, "tensor"),
        P(DP, "tensor"),
        P(DP, "tensor"),
        P(DP, None, "tensor"),
        P(DP, None, "tensor"),
        P(DP),
        P(rows, None),
        P("tensor", DP),
        P(),
        P(rows, None),
        P(rows, None),
        P(rows, None, None),
        P(rows, None, None),
        P(rows, None, None),
    )
    out_specs = (P(rows, None), P(rows, None))
    return jax.shard_map(
        shards, mesh=split_mesh, in_specs=in_specs, out_specs=out_specs, check_vma=False
    )
```

```python
import math

import jax
import jax.numpy as jnp
import numpy as np
from jax import lax
from jax.sharding import Mesh
from jax.sharding import PartitionSpec as P

HD = 128
DP = ("zh", "dl")
HALF = ("dl", "tensor")


def attend_local(query, new_key, new_value, cache_key, cache_value, lengths):
    row_count = query.shape[0]
    cache_len = cache_key.shape[1]
    kv_here = new_key.shape[1] // HD
    grouping = query.shape[1] // (kv_here * HD)
    queries = query.reshape(row_count, kv_here, grouping, HD)
    cache_keys = cache_key.reshape(row_count, cache_len, kv_here, HD)
    values = cache_value.reshape(row_count, cache_len, kv_here, HD)
    own_key = new_key.reshape(row_count, kv_here, HD)
    own_value = new_value.reshape(row_count, kv_here, HD)
    factor = 1.0 / math.sqrt(HD)
    scores = (
        jnp.einsum("rkgd,rckd->rkgc", queries, cache_keys, preferred_element_type=jnp.float32)
        * factor
    )
    own_score = (
        jnp.einsum("rkgd,rkd->rkg", queries, own_key, preferred_element_type=jnp.float32) * factor
    )
    visible = (jnp.arange(cache_len, dtype=jnp.int32)[None, :] < lengths[:, None])[:, None, None, :]
    highest = jnp.maximum(jnp.max(jnp.where(visible, scores, -1e30), axis=-1), own_score)
    exponent = jnp.where(visible, jnp.exp(scores - highest[..., None]), 0.0)
    own_exponent = jnp.exp(own_score - highest)
    totals = jnp.sum(exponent, axis=-1) + own_exponent
    probability = (exponent / totals[..., None]).astype(jnp.bfloat16)
    own_probability = (own_exponent / totals).astype(jnp.bfloat16)
    combined = jnp.einsum(
        "rkgc,rckd->rkgd", probability, values, preferred_element_type=jnp.float32
    )
    combined = (
        combined
        + own_probability.astype(jnp.float32)[..., None]
        * own_value.astype(jnp.float32)[:, :, None, :]
    )
    return combined.reshape(row_count, kv_here * grouping * HD).astype(jnp.bfloat16)


def swap_halves(x):
    return lax.ppermute(x, "zh", [(0, 1), (1, 0)])


def expert_layer(normed, route_ids, route_weight, w_gate, w_up, w_down):
    tok_here, width = normed.shape
    chosen_count = route_ids.shape[1]
    n_half = lax.axis_size("dl") * lax.axis_size("tensor")
    experts_all = 2 * n_half
    capacity = 2 * max(2, 3 * tok_here * chosen_count // experts_all)
    side = lax.axis_index("zh")
    other_rows = swap_halves(normed)
    other_ids = swap_halves(route_ids)
    other_weight = swap_halves(route_weight)
    first = side == 0
    rows = jnp.where(first, jnp.concatenate([normed, other_rows]), jnp.concatenate([other_rows, normed]))
    ids = jnp.where(first, jnp.concatenate([route_ids, other_ids]), jnp.concatenate([other_ids, route_ids]))
    weights = jnp.where(
        first,
        jnp.concatenate([route_weight, other_weight]),
        jnp.concatenate([other_weight, route_weight]),
    )
    held = 2 * tok_here
    pair_count = held * chosen_count
    local_ids = ids.reshape(pair_count) - side * n_half
    expert_hits = (local_ids[:, None] == jnp.arange(n_half, dtype=jnp.int32)[None, :]).astype(
        jnp.int32
    )
    earlier = jnp.cumsum(expert_hits, axis=0) - expert_hits
    slot_index = jnp.sum(earlier * expert_hits, axis=1)
    in_half = jnp.sum(expert_hits, axis=1) > 0
    target = jnp.where(in_half, local_ids * capacity + slot_index, -1)
    placement = (
        jnp.arange(n_half * capacity, dtype=jnp.int32)[:, None] == target[None, :]
    ).astype(jnp.bfloat16)
    token_place = jnp.sum(placement.reshape(n_half * capacity, held, chosen_count), axis=2)
    outgoing = jnp.dot(token_place, rows, preferred_element_type=jnp.float32).astype(jnp.bfloat16)
    outgoing = outgoing.reshape(n_half, capacity, width)
    received = lax.all_to_all(outgoing, HALF, split_axis=0, concat_axis=0, tiled=True)
    flat_rows = received.reshape(-1, width)
    gate_part = jnp.dot(flat_rows, w_gate[0], preferred_element_type=jnp.float32)
    up_part = jnp.dot(flat_rows, w_up[0], preferred_element_type=jnp.float32)
    activation = (jax.nn.silu(gate_part) * up_part).astype(jnp.bfloat16)
    result = jnp.dot(activation, w_down[0], preferred_element_type=jnp.float32).astype(jnp.bfloat16)
    returned = lax.all_to_all(
        result.reshape(received.shape), HALF, split_axis=0, concat_axis=0, tiled=True
    )
    returned = returned.reshape(n_half * capacity, width)
    pair_rows = jnp.einsum("sp,sd->pd", placement, returned, preferred_element_type=jnp.float32)
    weighted = weights[..., None] * pair_rows.reshape(held, chosen_count, width)
    partial = jnp.sum(weighted, axis=1)
    mine = jnp.where(first, partial[:tok_here], partial[tok_here:])
    theirs = jnp.where(first, partial[tok_here:], partial[:tok_here])
    return (mine + swap_halves(theirs)).astype(jnp.bfloat16)


def shards(
    query,
    new_key,
    new_value,
    cache_key,
    cache_value,
    lengths,
    hidden_in,
    out_weight,
    norm_gain,
    route_ids,
    route_weight,
    w_gate,
    w_up,
    w_down,
):
    heads_out = attend_local(query, new_key, new_value, cache_key, cache_value, lengths)
    n_dl = lax.axis_size("dl")
    n_t = lax.axis_size("tensor")
    tok_here = hidden_in.shape[0]
    first = lax.axis_index("zh") == 0
    other_heads = swap_halves(heads_out)
    pair_heads = jnp.where(
        first,
        jnp.concatenate([heads_out, other_heads]),
        jnp.concatenate([other_heads, heads_out]),
    )
    spread = jnp.broadcast_to(pair_heads[None], (n_dl,) + pair_heads.shape)
    gathered = lax.all_to_all(spread, "dl", split_axis=0, concat_axis=0, tiled=True)
    partial_cols = jnp.dot(
        gathered.reshape(-1, gathered.shape[-1]), out_weight, preferred_element_type=jnp.float32
    )
    col_width = partial_cols.shape[-1]
    by_dest = partial_cols.reshape(n_dl, 2, n_t, tok_here, col_width).transpose(1, 0, 2, 3, 4)
    by_dest = by_dest.reshape(2 * n_dl * n_t, tok_here, col_width)
    arrived = lax.all_to_all(by_dest, DP + ("tensor",), split_axis=0, concat_axis=0, tiled=True)
    summed = jnp.sum(arrived.reshape(2 * n_dl, n_t, tok_here, col_width), axis=1)
    summed = summed.transpose(1, 0, 2).reshape(tok_here, 2 * n_dl * col_width)
    attended = (hidden_in.astype(jnp.float32) + summed).astype(jnp.bfloat16)
    widened = attended.astype(jnp.float32)
    scaled = widened * lax.rsqrt(jnp.mean(widened * widened, axis=-1, keepdims=True) + 1e-06)
    normed = (scaled * norm_gain).astype(jnp.bfloat16)
    expert_mix = expert_layer(normed, route_ids, route_weight, w_gate, w_up, w_down)
    return (attended, expert_mix)


def solution(mesh):
    n_dp = mesh.shape["dp"]
    devices = np.asarray(mesh.devices).reshape(2, n_dp // 2, mesh.shape["tensor"])
    split_mesh = Mesh(devices, ("zh", "dl", "tensor"))
    rows = DP + ("tensor",)
    in_specs = (
        P(DP, "tensor"),
        P(DP, "tensor"),
        P(DP, "tensor"),
        P(DP, None, "tensor"),
        P(DP, None, "tensor"),
        P(DP),
        P(rows, None),
        P("tensor", DP),
        P(),
        P(rows, None),
        P(rows, None),
        P(rows, None, None),
        P(rows, None, None),
        P(rows, None, None),
    )
    out_specs = (P(rows, None), P(rows, None))
    return jax.shard_map(
        shards, mesh=split_mesh, in_specs=in_specs, out_specs=out_specs, check_vma=False
    )
```

```python
import math

import jax
import jax.numpy as jnp
import numpy as np
from jax import lax
from jax.sharding import Mesh
from jax.sharding import PartitionSpec as P

HD = 128
DP = ("zh", "dl")
HALF = ("dl", "tensor")


def attend_local(query, new_key, new_value, cache_key, cache_value, lengths):
    row_count = query.shape[0]
    cache_len = cache_key.shape[1]
    kv_here = new_key.shape[1] // HD
    grouping = query.shape[1] // (kv_here * HD)
    queries = query.reshape(row_count, kv_here, grouping, HD)
    cache_keys = cache_key.reshape(row_count, cache_len, kv_here, HD)
    values = cache_value.reshape(row_count, cache_len, kv_here, HD)
    own_key = new_key.reshape(row_count, kv_here, HD)
    own_value = new_value.reshape(row_count, kv_here, HD)
    factor = 1.0 / math.sqrt(HD)
    scores = (
        jnp.einsum("rkgd,rckd->rkgc", queries, cache_keys, preferred_element_type=jnp.float32)
        * factor
    )
    own_score = (
        jnp.einsum("rkgd,rkd->rkg", queries, own_key, preferred_element_type=jnp.float32) * factor
    )
    visible = (jnp.arange(cache_len, dtype=jnp.int32)[None, :] < lengths[:, None])[:, None, None, :]
    highest = jnp.maximum(jnp.max(jnp.where(visible, scores, -1e30), axis=-1), own_score)
    exponent = jnp.where(visible, jnp.exp(scores - highest[..., None]), 0.0)
    own_exponent = jnp.exp(own_score - highest)
    totals = jnp.sum(exponent, axis=-1) + own_exponent
    probability = (exponent / totals[..., None]).astype(jnp.bfloat16)
    own_probability = (own_exponent / totals).astype(jnp.bfloat16)
    combined = jnp.einsum(
        "rkgc,rckd->rkgd", probability, values, preferred_element_type=jnp.float32
    )
    combined = (
        combined
        + own_probability.astype(jnp.float32)[..., None]
        * own_value.astype(jnp.float32)[:, :, None, :]
    )
    return combined.reshape(row_count, kv_here * grouping * HD).astype(jnp.bfloat16)


def swap_halves(x):
    return lax.ppermute(x, "zh", [(0, 1), (1, 0)])


def expert_layer(normed, route_ids, route_weight, w_gate, w_up, w_down):
    tok_here, width = normed.shape
    chosen_count = route_ids.shape[1]
    n_half = lax.axis_size("dl") * lax.axis_size("tensor")
    experts_all = 2 * n_half
    capacity = 2 * max(2, 3 * tok_here * chosen_count // experts_all)
    side = lax.axis_index("zh")
    other_rows = swap_halves(normed)
    other_ids = swap_halves(route_ids)
    other_weight = swap_halves(route_weight)
    first = side == 0
    rows = jnp.where(first, jnp.concatenate([normed, other_rows]), jnp.concatenate([other_rows, normed]))
    ids = jnp.where(first, jnp.concatenate([route_ids, other_ids]), jnp.concatenate([other_ids, route_ids]))
    weights = jnp.where(
        first,
        jnp.concatenate([route_weight, other_weight]),
        jnp.concatenate([other_weight, route_weight]),
    )
    held = 2 * tok_here
    pair_count = held * chosen_count
    local_ids = ids.reshape(pair_count) - side * n_half
    expert_hits = (local_ids[:, None] == jnp.arange(n_half, dtype=jnp.int32)[None, :]).astype(
        jnp.int32
    )
    earlier = jnp.cumsum(expert_hits, axis=0) - expert_hits
    slot_index = jnp.sum(earlier * expert_hits, axis=1)
    in_half = jnp.sum(expert_hits, axis=1) > 0
    target = jnp.where(in_half, local_ids * capacity + slot_index, -1)
    placement = (
        jnp.arange(n_half * capacity, dtype=jnp.int32)[:, None] == target[None, :]
    ).astype(jnp.bfloat16)
    token_place = jnp.sum(placement.reshape(n_half, capacity, held, chosen_count), axis=3)
    outgoing = jnp.einsum(
        "hcp,pd->hcd", token_place, rows, preferred_element_type=jnp.float32
    ).astype(jnp.bfloat16)
    received = lax.all_to_all(outgoing, HALF, split_axis=0, concat_axis=0, tiled=True)
    gate_part = jnp.einsum("hcd,df->hcf", received, w_gate[0], preferred_element_type=jnp.float32)
    up_part = jnp.einsum("hcd,df->hcf", received, w_up[0], preferred_element_type=jnp.float32)
    activation = (jax.nn.silu(gate_part) * up_part).astype(jnp.bfloat16)
    result = jnp.einsum(
        "hcf,fd->hcd", activation, w_down[0], preferred_element_type=jnp.float32
    ).astype(jnp.bfloat16)
    returned = lax.all_to_all(result, HALF, split_axis=0, concat_axis=0, tiled=True)
    pair_rows = jnp.einsum(
        "hcp,hcd->pd",
        placement.reshape(n_half, capacity, pair_count),
        returned,
        preferred_element_type=jnp.float32,
    )
    weighted = weights[..., None] * pair_rows.reshape(held, chosen_count, width)
    partial = jnp.sum(weighted, axis=1)
    mine = jnp.where(first, partial[:tok_here], partial[tok_here:])
    theirs = jnp.where(first, partial[tok_here:], partial[:tok_here])
    return (mine + swap_halves(theirs)).astype(jnp.bfloat16)


def shards(
    query,
    new_key,
    new_value,
    cache_key,
    cache_value,
    lengths,
    hidden_in,
    out_weight,
    norm_gain,
    route_ids,
    route_weight,
    w_gate,
    w_up,
    w_down,
):
    heads_out = attend_local(query, new_key, new_value, cache_key, cache_value, lengths)
    n_dl = lax.axis_size("dl")
    n_t = lax.axis_size("tensor")
    tok_here = hidden_in.shape[0]
    first = lax.axis_index("zh") == 0
    other_heads = swap_halves(heads_out)
    pair_heads = jnp.where(
        first,
        jnp.concatenate([heads_out, other_heads]),
        jnp.concatenate([other_heads, heads_out]),
    )
    spread = jnp.broadcast_to(pair_heads[None], (n_dl,) + pair_heads.shape)
    gathered = lax.all_to_all(spread, "dl", split_axis=0, concat_axis=0, tiled=True)
    partial_cols = jnp.dot(
        gathered.reshape(-1, gathered.shape[-1]), out_weight, preferred_element_type=jnp.float32
    )
    col_width = partial_cols.shape[-1]
    by_dest = partial_cols.reshape(n_dl, 2, n_t, tok_here, col_width).transpose(1, 0, 2, 3, 4)
    by_dest = by_dest.reshape(2 * n_dl * n_t, tok_here, col_width)
    arrived = lax.all_to_all(by_dest, DP + ("tensor",), split_axis=0, concat_axis=0, tiled=True)
    summed = jnp.sum(arrived.reshape(2 * n_dl, n_t, tok_here, col_width), axis=1)
    summed = summed.transpose(1, 0, 2).reshape(tok_here, 2 * n_dl * col_width)
    attended = (hidden_in.astype(jnp.float32) + summed).astype(jnp.bfloat16)
    widened = attended.astype(jnp.float32)
    scaled = widened * lax.rsqrt(jnp.mean(widened * widened, axis=-1, keepdims=True) + 1e-06)
    normed = (scaled * norm_gain).astype(jnp.bfloat16)
    expert_mix = expert_layer(normed, route_ids, route_weight, w_gate, w_up, w_down)
    return (attended, expert_mix)


def solution(mesh):
    n_dp = mesh.shape["dp"]
    devices = np.asarray(mesh.devices).reshape(2, n_dp // 2, mesh.shape["tensor"])
    split_mesh = Mesh(devices, ("zh", "dl", "tensor"))
    rows = DP + ("tensor",)
    in_specs = (
        P(DP, "tensor"),
        P(DP, "tensor"),
        P(DP, "tensor"),
        P(DP, None, "tensor"),
        P(DP, None, "tensor"),
        P(DP),
        P(rows, None),
        P("tensor", DP),
        P(),
        P(rows, None),
        P(rows, None),
        P(rows, None, None),
        P(rows, None, None),
        P(rows, None, None),
    )
    out_specs = (P(rows, None), P(rows, None))
    return jax.shard_map(
        shards, mesh=split_mesh, in_specs=in_specs, out_specs=out_specs, check_vma=False
    )
```

```python
import math

import jax
import jax.numpy as jnp
import numpy as np
from jax import lax
from jax.sharding import Mesh
from jax.sharding import PartitionSpec as P

HD = 128
DP = ("zh", "dl")
HALF = ("dl", "tensor")


def attend_local(query, new_key, new_value, cache_key, cache_value, lengths):
    row_count = query.shape[0]
    cache_len = cache_key.shape[1]
    kv_here = new_key.shape[1] // HD
    grouping = query.shape[1] // (kv_here * HD)
    queries = query.reshape(row_count, kv_here, grouping, HD)
    cache_keys = cache_key.reshape(row_count, cache_len, kv_here, HD)
    values = cache_value.reshape(row_count, cache_len, kv_here, HD)
    own_key = new_key.reshape(row_count, kv_here, HD)
    own_value = new_value.reshape(row_count, kv_here, HD)
    factor = 1.0 / math.sqrt(HD)
    scores = (
        jnp.einsum("rkgd,rckd->rkgc", queries, cache_keys, preferred_element_type=jnp.float32)
        * factor
    )
    own_score = (
        jnp.einsum("rkgd,rkd->rkg", queries, own_key, preferred_element_type=jnp.float32) * factor
    )
    visible = (jnp.arange(cache_len, dtype=jnp.int32)[None, :] < lengths[:, None])[:, None, None, :]
    highest = jnp.maximum(jnp.max(jnp.where(visible, scores, -1e30), axis=-1), own_score)
    exponent = jnp.where(visible, jnp.exp(scores - highest[..., None]), 0.0)
    own_exponent = jnp.exp(own_score - highest)
    totals = jnp.sum(exponent, axis=-1) + own_exponent
    probability = (exponent / totals[..., None]).astype(jnp.bfloat16)
    own_probability = (own_exponent / totals).astype(jnp.bfloat16)
    combined = jnp.einsum(
        "rkgc,rckd->rkgd", probability, values, preferred_element_type=jnp.float32
    )
    combined = (
        combined
        + own_probability.astype(jnp.float32)[..., None]
        * own_value.astype(jnp.float32)[:, :, None, :]
    )
    return combined.reshape(row_count, kv_here * grouping * HD).astype(jnp.bfloat16)


def swap_halves(x):
    return lax.ppermute(x, "zh", [(0, 1), (1, 0)])


def expert_layer(normed, route_ids, route_weight, w_gate, w_up, w_down):
    tok_here, width = normed.shape
    chosen_count = route_ids.shape[1]
    n_half = lax.axis_size("dl") * lax.axis_size("tensor")
    experts_all = 2 * n_half
    capacity = 2 * max(2, 3 * tok_here * chosen_count // experts_all)
    side = lax.axis_index("zh")
    other_rows = swap_halves(normed)
    other_ids = swap_halves(route_ids)
    other_weight = swap_halves(route_weight)
    first = side == 0
    rows = jnp.where(first, jnp.concatenate([normed, other_rows]), jnp.concatenate([other_rows, normed]))
    ids = jnp.where(first, jnp.concatenate([route_ids, other_ids]), jnp.concatenate([other_ids, route_ids]))
    weights = jnp.where(
        first,
        jnp.concatenate([route_weight, other_weight]),
        jnp.concatenate([other_weight, route_weight]),
    )
    held = 2 * tok_here
    pair_count = held * chosen_count
    local_ids = ids.reshape(pair_count) - side * n_half
    expert_hits = (local_ids[:, None] == jnp.arange(n_half, dtype=jnp.int32)[None, :]).astype(
        jnp.int32
    )
    earlier = jnp.cumsum(expert_hits, axis=0) - expert_hits
    slot_index = jnp.sum(earlier * expert_hits, axis=1)
    in_half = jnp.sum(expert_hits, axis=1) > 0
    target = jnp.where(in_half, local_ids * capacity + slot_index, -1)
    placement = (
        jnp.arange(n_half * capacity, dtype=jnp.int32)[:, None] == target[None, :]
    ).astype(jnp.bfloat16)
    token_place = jnp.sum(placement.reshape(n_half, capacity, held, chosen_count), axis=3)
    outgoing = jnp.einsum(
        "hcp,pd->hcd", token_place, rows, preferred_element_type=jnp.float32
    ).astype(jnp.bfloat16)
    received = lax.all_to_all(outgoing, HALF, split_axis=0, concat_axis=0, tiled=True)
    gate_part = jnp.einsum("hcd,df->hcf", received, w_gate[0], preferred_element_type=jnp.float32)
    up_part = jnp.einsum("hcd,df->hcf", received, w_up[0], preferred_element_type=jnp.float32)
    activation = (jax.nn.silu(gate_part) * up_part).astype(jnp.bfloat16)
    result = jnp.einsum(
        "hcf,fd->hcd", activation, w_down[0], preferred_element_type=jnp.float32
    ).astype(jnp.bfloat16)
    returned = lax.all_to_all(result, HALF, split_axis=0, concat_axis=0, tiled=True)
    pair_rows = jnp.einsum(
        "hcp,hcd->pd",
        placement.reshape(n_half, capacity, pair_count),
        returned,
        preferred_element_type=jnp.float32,
    )
    weighted = weights[..., None] * pair_rows.reshape(held, chosen_count, width)
    partial = jnp.sum(weighted, axis=1)
    mine = jnp.where(first, partial[:tok_here], partial[tok_here:])
    theirs = jnp.where(first, partial[tok_here:], partial[:tok_here])
    sent = swap_halves(theirs.astype(jnp.bfloat16)).astype(jnp.float32)
    return (mine + sent).astype(jnp.bfloat16)


def shards(
    query,
    new_key,
    new_value,
    cache_key,
    cache_value,
    lengths,
    hidden_in,
    out_weight,
    norm_gain,
    route_ids,
    route_weight,
    w_gate,
    w_up,
    w_down,
):
    heads_out = attend_local(query, new_key, new_value, cache_key, cache_value, lengths)
    n_dl = lax.axis_size("dl")
    n_t = lax.axis_size("tensor")
    tok_here = hidden_in.shape[0]
    first = lax.axis_index("zh") == 0
    other_heads = swap_halves(heads_out)
    pair_heads = jnp.where(
        first,
        jnp.concatenate([heads_out, other_heads]),
        jnp.concatenate([other_heads, heads_out]),
    )
    spread = jnp.broadcast_to(pair_heads[None], (n_dl,) + pair_heads.shape)
    gathered = lax.all_to_all(spread, "dl", split_axis=0, concat_axis=0, tiled=True)
    partial_cols = jnp.dot(
        gathered.reshape(-1, gathered.shape[-1]), out_weight, preferred_element_type=jnp.float32
    )
    col_width = partial_cols.shape[-1]
    by_dest = partial_cols.reshape(n_dl, 2, n_t, tok_here, col_width).transpose(1, 0, 2, 3, 4)
    by_dest = by_dest.reshape(2 * n_dl * n_t, tok_here, col_width)
    arrived = lax.all_to_all(
        by_dest.astype(jnp.bfloat16), DP + ("tensor",), split_axis=0, concat_axis=0, tiled=True
    )
    arrived = arrived.astype(jnp.float32).reshape(2 * n_dl, n_t, tok_here, col_width)
    summed = jnp.sum(arrived, axis=1)
    summed = summed.transpose(1, 0, 2).reshape(tok_here, 2 * n_dl * col_width)
    attended = (hidden_in.astype(jnp.float32) + summed).astype(jnp.bfloat16)
    widened = attended.astype(jnp.float32)
    scaled = widened * lax.rsqrt(jnp.mean(widened * widened, axis=-1, keepdims=True) + 1e-06)
    normed = (scaled * norm_gain).astype(jnp.bfloat16)
    expert_mix = expert_layer(normed, route_ids, route_weight, w_gate, w_up, w_down)
    return (attended, expert_mix)


def solution(mesh):
    n_dp = mesh.shape["dp"]
    devices = np.asarray(mesh.devices).reshape(2, n_dp // 2, mesh.shape["tensor"])
    split_mesh = Mesh(devices, ("zh", "dl", "tensor"))
    rows = DP + ("tensor",)
    in_specs = (
        P(DP, "tensor"),
        P(DP, "tensor"),
        P(DP, "tensor"),
        P(DP, None, "tensor"),
        P(DP, None, "tensor"),
        P(DP),
        P(rows, None),
        P("tensor", DP),
        P(),
        P(rows, None),
        P(rows, None),
        P(rows, None, None),
        P(rows, None, None),
        P(rows, None, None),
    )
    out_specs = (P(rows, None), P(rows, None))
    return jax.shard_map(
        shards, mesh=split_mesh, in_specs=in_specs, out_specs=out_specs, check_vma=False
    )
```

```python
import math

import jax
import jax.numpy as jnp
import numpy as np
from jax import lax
from jax.sharding import Mesh
from jax.sharding import PartitionSpec as P

HD = 128
DP = ("zh", "dl")
HALF = ("dl", "tensor")


def attend_local(query, new_key, new_value, cache_key, cache_value, lengths):
    row_count = query.shape[0]
    cache_len = cache_key.shape[1]
    kv_here = new_key.shape[1] // HD
    grouping = query.shape[1] // (kv_here * HD)
    queries = query.reshape(row_count, kv_here, grouping, HD)
    cache_keys = cache_key.reshape(row_count, cache_len, kv_here, HD)
    values = cache_value.reshape(row_count, cache_len, kv_here, HD)
    own_key = new_key.reshape(row_count, kv_here, HD)
    own_value = new_value.reshape(row_count, kv_here, HD)
    factor = 1.0 / math.sqrt(HD)
    scores = (
        jnp.einsum("rkgd,rckd->rkgc", queries, cache_keys, preferred_element_type=jnp.float32)
        * factor
    )
    own_score = (
        jnp.einsum("rkgd,rkd->rkg", queries, own_key, preferred_element_type=jnp.float32) * factor
    )
    visible = (jnp.arange(cache_len, dtype=jnp.int32)[None, :] < lengths[:, None])[:, None, None, :]
    highest = jnp.maximum(jnp.max(jnp.where(visible, scores, -1e30), axis=-1), own_score)
    exponent = jnp.where(visible, jnp.exp(scores - highest[..., None]), 0.0)
    own_exponent = jnp.exp(own_score - highest)
    totals = jnp.sum(exponent, axis=-1) + own_exponent
    probability = (exponent / totals[..., None]).astype(jnp.bfloat16)
    own_probability = (own_exponent / totals).astype(jnp.bfloat16)
    combined = jnp.einsum(
        "rkgc,rckd->rkgd", probability, values, preferred_element_type=jnp.float32
    )
    combined = (
        combined
        + own_probability.astype(jnp.float32)[..., None]
        * own_value.astype(jnp.float32)[:, :, None, :]
    )
    return combined.reshape(row_count, kv_here * grouping * HD).astype(jnp.bfloat16)


def swap_halves(x):
    return lax.ppermute(x, "zh", [(0, 1), (1, 0)])


def expert_layer(normed, route_ids, route_weight, w_gate, w_up, w_down):
    tok_here, width = normed.shape
    chosen_count = route_ids.shape[1]
    n_half = lax.axis_size("dl") * lax.axis_size("tensor")
    experts_all = 2 * n_half
    capacity = 2 * max(2, 3 * tok_here * chosen_count // experts_all)
    side = lax.axis_index("zh")
    other_rows = swap_halves(normed)
    packed = swap_halves(jnp.concatenate([route_ids.astype(jnp.float32), route_weight], axis=1))
    other_ids = packed[:, :chosen_count].astype(jnp.int32)
    other_weight = packed[:, chosen_count:]
    first = side == 0
    rows = jnp.where(first, jnp.concatenate([normed, other_rows]), jnp.concatenate([other_rows, normed]))
    ids = jnp.where(first, jnp.concatenate([route_ids, other_ids]), jnp.concatenate([other_ids, route_ids]))
    weights = jnp.where(
        first,
        jnp.concatenate([route_weight, other_weight]),
        jnp.concatenate([other_weight, route_weight]),
    )
    held = 2 * tok_here
    pair_count = held * chosen_count
    local_ids = ids.reshape(pair_count) - side * n_half
    expert_hits = (local_ids[:, None] == jnp.arange(n_half, dtype=jnp.int32)[None, :]).astype(
        jnp.int32
    )
    earlier = jnp.cumsum(expert_hits, axis=0) - expert_hits
    slot_index = jnp.sum(earlier * expert_hits, axis=1)
    in_half = jnp.sum(expert_hits, axis=1) > 0
    target = jnp.where(in_half, local_ids * capacity + slot_index, -1)
    placement = (
        jnp.arange(n_half * capacity, dtype=jnp.int32)[:, None] == target[None, :]
    ).astype(jnp.bfloat16)
    token_place = jnp.sum(placement.reshape(n_half, capacity, held, chosen_count), axis=3)
    outgoing = jnp.einsum(
        "hcp,pd->hcd", token_place, rows, preferred_element_type=jnp.float32
    ).astype(jnp.bfloat16)
    received = lax.all_to_all(outgoing, HALF, split_axis=0, concat_axis=0, tiled=True)
    gate_part = jnp.einsum("hcd,df->hcf", received, w_gate[0], preferred_element_type=jnp.float32)
    up_part = jnp.einsum("hcd,df->hcf", received, w_up[0], preferred_element_type=jnp.float32)
    activation = (jax.nn.silu(gate_part) * up_part).astype(jnp.bfloat16)
    result = jnp.einsum(
        "hcf,fd->hcd", activation, w_down[0], preferred_element_type=jnp.float32
    ).astype(jnp.bfloat16)
    returned = lax.all_to_all(result, HALF, split_axis=0, concat_axis=0, tiled=True)
    pair_rows = jnp.einsum(
        "hcp,hcd->pd",
        placement.reshape(n_half, capacity, pair_count),
        returned,
        preferred_element_type=jnp.float32,
    )
    weighted = weights[..., None] * pair_rows.reshape(held, chosen_count, width)
    partial = jnp.sum(weighted, axis=1)
    mine = jnp.where(first, partial[:tok_here], partial[tok_here:])
    theirs = jnp.where(first, partial[tok_here:], partial[:tok_here])
    sent = swap_halves(theirs.astype(jnp.bfloat16)).astype(jnp.float32)
    return (mine + sent).astype(jnp.bfloat16)


def shards(
    query,
    new_key,
    new_value,
    cache_key,
    cache_value,
    lengths,
    hidden_in,
    out_weight,
    norm_gain,
    route_ids,
    route_weight,
    w_gate,
    w_up,
    w_down,
):
    heads_out = attend_local(query, new_key, new_value, cache_key, cache_value, lengths)
    n_dl = lax.axis_size("dl")
    n_t = lax.axis_size("tensor")
    tok_here = hidden_in.shape[0]
    first = lax.axis_index("zh") == 0
    other_heads = swap_halves(heads_out)
    pair_heads = jnp.where(
        first,
        jnp.concatenate([heads_out, other_heads]),
        jnp.concatenate([other_heads, heads_out]),
    )
    spread = jnp.broadcast_to(pair_heads[None], (n_dl,) + pair_heads.shape)
    gathered = lax.all_to_all(spread, "dl", split_axis=0, concat_axis=0, tiled=True)
    partial_cols = jnp.einsum(
        "sqd,df->sqf", gathered, out_weight, preferred_element_type=jnp.float32
    )
    col_width = partial_cols.shape[-1]
    by_dest = partial_cols.reshape(n_dl, 2, n_t, tok_here, col_width).transpose(1, 0, 2, 3, 4)
    by_dest = by_dest.reshape(2 * n_dl * n_t, tok_here, col_width)
    arrived = lax.all_to_all(
        by_dest.astype(jnp.bfloat16), DP + ("tensor",), split_axis=0, concat_axis=0, tiled=True
    )
    arrived = arrived.astype(jnp.float32).reshape(2 * n_dl, n_t, tok_here, col_width)
    summed = jnp.sum(arrived, axis=1)
    summed = summed.transpose(1, 0, 2).reshape(tok_here, 2 * n_dl * col_width)
    attended = (hidden_in.astype(jnp.float32) + summed).astype(jnp.bfloat16)
    widened = attended.astype(jnp.float32)
    scaled = widened * lax.rsqrt(jnp.mean(widened * widened, axis=-1, keepdims=True) + 1e-06)
    normed = (scaled * norm_gain).astype(jnp.bfloat16)
    expert_mix = expert_layer(normed, route_ids, route_weight, w_gate, w_up, w_down)
    return (attended, expert_mix)


def solution(mesh):
    n_dp = mesh.shape["dp"]
    devices = np.asarray(mesh.devices).reshape(2, n_dp // 2, mesh.shape["tensor"])
    split_mesh = Mesh(devices, ("zh", "dl", "tensor"))
    rows = DP + ("tensor",)
    in_specs = (
        P(DP, "tensor"),
        P(DP, "tensor"),
        P(DP, "tensor"),
        P(DP, None, "tensor"),
        P(DP, None, "tensor"),
        P(DP),
        P(rows, None),
        P("tensor", DP),
        P(),
        P(rows, None),
        P(rows, None),
        P(rows, None, None),
        P(rows, None, None),
        P(rows, None, None),
    )
    out_specs = (P(rows, None), P(rows, None))
    return jax.shard_map(
        shards, mesh=split_mesh, in_specs=in_specs, out_specs=out_specs, check_vma=False
    )
```

```python
import math

import jax
import jax.numpy as jnp
import numpy as np
from jax import lax
from jax.sharding import Mesh
from jax.sharding import PartitionSpec as P

HD = 128
DP = ("zh", "dl")
HALF = ("dl", "tensor")


def attend_local(query, new_key, new_value, cache_key, cache_value, lengths):
    row_count = query.shape[0]
    cache_len = cache_key.shape[1]
    kv_here = new_key.shape[1] // HD
    grouping = query.shape[1] // (kv_here * HD)
    queries = query.reshape(row_count, kv_here, grouping, HD)
    cache_keys = cache_key.reshape(row_count, cache_len, kv_here, HD)
    values = cache_value.reshape(row_count, cache_len, kv_here, HD)
    own_key = new_key.reshape(row_count, kv_here, HD)
    own_value = new_value.reshape(row_count, kv_here, HD)
    factor = 1.0 / math.sqrt(HD)
    scores = (
        jnp.einsum("rkgd,rckd->rkgc", queries, cache_keys, preferred_element_type=jnp.float32)
        * factor
    )
    own_score = (
        jnp.einsum("rkgd,rkd->rkg", queries, own_key, preferred_element_type=jnp.float32) * factor
    )
    visible = (jnp.arange(cache_len, dtype=jnp.int32)[None, :] < lengths[:, None])[:, None, None, :]
    highest = jnp.maximum(jnp.max(jnp.where(visible, scores, -1e30), axis=-1), own_score)
    exponent = jnp.where(visible, jnp.exp(scores - highest[..., None]), 0.0)
    own_exponent = jnp.exp(own_score - highest)
    totals = jnp.sum(exponent, axis=-1) + own_exponent
    probability = (exponent / totals[..., None]).astype(jnp.bfloat16)
    own_probability = (own_exponent / totals).astype(jnp.bfloat16)
    combined = jnp.einsum(
        "rkgc,rckd->rkgd", probability, values, preferred_element_type=jnp.float32
    )
    combined = (
        combined
        + own_probability.astype(jnp.float32)[..., None]
        * own_value.astype(jnp.float32)[:, :, None, :]
    )
    return combined.reshape(row_count, kv_here * grouping * HD).astype(jnp.bfloat16)


def swap_halves(x):
    return lax.ppermute(x, "zh", [(0, 1), (1, 0)])


def expert_layer(normed, route_ids, route_weight, w_gate, w_up, w_down):
    tok_here, width = normed.shape
    chosen_count = route_ids.shape[1]
    n_half = lax.axis_size("dl") * lax.axis_size("tensor")
    experts_all = 2 * n_half
    capacity = 2 * max(2, 3 * tok_here * chosen_count // experts_all)
    capacity = -(-capacity // 8) * 8
    side = lax.axis_index("zh")
    other_rows = swap_halves(normed)
    packed = swap_halves(jnp.concatenate([route_ids.astype(jnp.float32), route_weight], axis=1))
    other_ids = packed[:, :chosen_count].astype(jnp.int32)
    other_weight = packed[:, chosen_count:]
    first = side == 0
    rows = jnp.where(first, jnp.concatenate([normed, other_rows]), jnp.concatenate([other_rows, normed]))
    ids = jnp.where(first, jnp.concatenate([route_ids, other_ids]), jnp.concatenate([other_ids, route_ids]))
    weights = jnp.where(
        first,
        jnp.concatenate([route_weight, other_weight]),
        jnp.concatenate([other_weight, route_weight]),
    )
    held = 2 * tok_here
    pair_count = held * chosen_count
    local_ids = ids.reshape(pair_count) - side * n_half
    expert_hits = (local_ids[:, None] == jnp.arange(n_half, dtype=jnp.int32)[None, :]).astype(
        jnp.int32
    )
    earlier = jnp.cumsum(expert_hits, axis=0) - expert_hits
    slot_index = jnp.sum(earlier * expert_hits, axis=1)
    in_half = jnp.sum(expert_hits, axis=1) > 0
    target = jnp.where(in_half, local_ids * capacity + slot_index, -1)
    placement = (
        jnp.arange(n_half * capacity, dtype=jnp.int32)[:, None] == target[None, :]
    ).astype(jnp.bfloat16)
    token_place = jnp.sum(placement.reshape(n_half, capacity, held, chosen_count), axis=3)
    outgoing = jnp.einsum(
        "hcp,pd->hcd", token_place, rows, preferred_element_type=jnp.float32
    ).astype(jnp.bfloat16)
    received = lax.all_to_all(outgoing, HALF, split_axis=0, concat_axis=0, tiled=True)
    gate_part = jnp.einsum("hcd,df->hcf", received, w_gate[0], preferred_element_type=jnp.float32)
    up_part = jnp.einsum("hcd,df->hcf", received, w_up[0], preferred_element_type=jnp.float32)
    activation = (jax.nn.silu(gate_part) * up_part).astype(jnp.bfloat16)
    result = jnp.einsum(
        "hcf,fd->hcd", activation, w_down[0], preferred_element_type=jnp.float32
    ).astype(jnp.bfloat16)
    returned = lax.all_to_all(result, HALF, split_axis=0, concat_axis=0, tiled=True)
    pair_rows = jnp.einsum(
        "hcp,hcd->pd",
        placement.reshape(n_half, capacity, pair_count),
        returned,
        preferred_element_type=jnp.float32,
    )
    weighted = weights[..., None] * pair_rows.reshape(held, chosen_count, width)
    partial = jnp.sum(weighted, axis=1)
    mine = jnp.where(first, partial[:tok_here], partial[tok_here:])
    theirs = jnp.where(first, partial[tok_here:], partial[:tok_here])
    sent = swap_halves(theirs.astype(jnp.bfloat16)).astype(jnp.float32)
    return (mine + sent).astype(jnp.bfloat16)


def shards(
    query,
    new_key,
    new_value,
    cache_key,
    cache_value,
    lengths,
    hidden_in,
    out_weight,
    norm_gain,
    route_ids,
    route_weight,
    w_gate,
    w_up,
    w_down,
):
    heads_out = attend_local(query, new_key, new_value, cache_key, cache_value, lengths)
    n_dl = lax.axis_size("dl")
    n_t = lax.axis_size("tensor")
    tok_here = hidden_in.shape[0]
    first = lax.axis_index("zh") == 0
    other_heads = swap_halves(heads_out)
    pair_heads = jnp.where(
        first,
        jnp.concatenate([heads_out, other_heads]),
        jnp.concatenate([other_heads, heads_out]),
    )
    spread = jnp.broadcast_to(pair_heads[None], (n_dl,) + pair_heads.shape)
    gathered = lax.all_to_all(spread, "dl", split_axis=0, concat_axis=0, tiled=True)
    partial_cols = jnp.einsum(
        "sqd,df->sqf", gathered, out_weight, preferred_element_type=jnp.float32
    )
    col_width = partial_cols.shape[-1]
    by_dest = partial_cols.reshape(n_dl, 2, n_t, tok_here, col_width).transpose(1, 0, 2, 3, 4)
    by_dest = by_dest.reshape(2 * n_dl * n_t, tok_here, col_width)
    arrived = lax.all_to_all(
        by_dest.astype(jnp.bfloat16), DP + ("tensor",), split_axis=0, concat_axis=0, tiled=True
    )
    arrived = arrived.astype(jnp.float32).reshape(2 * n_dl, n_t, tok_here, col_width)
    summed = jnp.sum(arrived, axis=1)
    summed = summed.transpose(1, 0, 2).reshape(tok_here, 2 * n_dl * col_width)
    attended = (hidden_in.astype(jnp.float32) + summed).astype(jnp.bfloat16)
    widened = attended.astype(jnp.float32)
    scaled = widened * lax.rsqrt(jnp.mean(widened * widened, axis=-1, keepdims=True) + 1e-06)
    normed = (scaled * norm_gain).astype(jnp.bfloat16)
    expert_mix = expert_layer(normed, route_ids, route_weight, w_gate, w_up, w_down)
    return (attended, expert_mix)


def solution(mesh):
    n_dp = mesh.shape["dp"]
    devices = np.asarray(mesh.devices).reshape(2, n_dp // 2, mesh.shape["tensor"])
    split_mesh = Mesh(devices, ("zh", "dl", "tensor"))
    rows = DP + ("tensor",)
    in_specs = (
        P(DP, "tensor"),
        P(DP, "tensor"),
        P(DP, "tensor"),
        P(DP, None, "tensor"),
        P(DP, None, "tensor"),
        P(DP),
        P(rows, None),
        P("tensor", DP),
        P(),
        P(rows, None),
        P(rows, None),
        P(rows, None, None),
        P(rows, None, None),
        P(rows, None, None),
    )
    out_specs = (P(rows, None), P(rows, None))
    return jax.shard_map(
        shards, mesh=split_mesh, in_specs=in_specs, out_specs=out_specs, check_vma=False
    )
```

```python
import math

import jax
import jax.numpy as jnp
import numpy as np
from jax import lax
from jax.sharding import Mesh
from jax.sharding import PartitionSpec as P

HD = 128
DP = ("zh", "dl")
HALF = ("dl", "tensor")


def attend_local(query, new_key, new_value, cache_key, cache_value, lengths):
    row_count = query.shape[0]
    cache_len = cache_key.shape[1]
    kv_here = new_key.shape[1] // HD
    grouping = query.shape[1] // (kv_here * HD)
    queries = query.reshape(row_count, kv_here, grouping, HD)
    cache_keys = cache_key.reshape(row_count, cache_len, kv_here, HD)
    values = cache_value.reshape(row_count, cache_len, kv_here, HD)
    own_key = new_key.reshape(row_count, kv_here, HD)
    own_value = new_value.reshape(row_count, kv_here, HD)
    factor = 1.0 / math.sqrt(HD)
    scores = (
        jnp.einsum("rkgd,rckd->rkgc", queries, cache_keys, preferred_element_type=jnp.float32)
        * factor
    )
    own_score = (
        jnp.einsum("rkgd,rkd->rkg", queries, own_key, preferred_element_type=jnp.float32) * factor
    )
    visible = (jnp.arange(cache_len, dtype=jnp.int32)[None, :] < lengths[:, None])[:, None, None, :]
    highest = jnp.maximum(jnp.max(jnp.where(visible, scores, -1e30), axis=-1), own_score)
    exponent = jnp.where(visible, jnp.exp(scores - highest[..., None]), 0.0)
    own_exponent = jnp.exp(own_score - highest)
    totals = jnp.sum(exponent, axis=-1) + own_exponent
    probability = (exponent / totals[..., None]).astype(jnp.bfloat16)
    own_probability = (own_exponent / totals).astype(jnp.bfloat16)
    combined = jnp.einsum(
        "rkgc,rckd->rkgd", probability, values, preferred_element_type=jnp.float32
    )
    combined = (
        combined
        + own_probability.astype(jnp.float32)[..., None]
        * own_value.astype(jnp.float32)[:, :, None, :]
    )
    return combined.reshape(row_count, kv_here * grouping * HD).astype(jnp.bfloat16)


def swap_halves(x):
    return lax.ppermute(x, "zh", [(0, 1), (1, 0)])


def expert_layer(normed, route_ids, route_weight, w_gate, w_up, w_down):
    tok_here, width = normed.shape
    chosen_count = route_ids.shape[1]
    n_half = lax.axis_size("dl") * lax.axis_size("tensor")
    experts_all = 2 * n_half
    capacity = 2 * max(2, 3 * tok_here * chosen_count // experts_all)
    capacity = -(-capacity // 8) * 8
    side = lax.axis_index("zh")
    other_rows = swap_halves(normed)
    packed = swap_halves(jnp.concatenate([route_ids.astype(jnp.float32), route_weight], axis=1))
    other_ids = packed[:, :chosen_count].astype(jnp.int32)
    other_weight = packed[:, chosen_count:]
    first = side == 0
    rows = jnp.where(first, jnp.concatenate([normed, other_rows]), jnp.concatenate([other_rows, normed]))
    ids = jnp.where(first, jnp.concatenate([route_ids, other_ids]), jnp.concatenate([other_ids, route_ids]))
    weights = jnp.where(
        first,
        jnp.concatenate([route_weight, other_weight]),
        jnp.concatenate([other_weight, route_weight]),
    )
    held = 2 * tok_here
    pair_count = held * chosen_count
    local_ids = ids.reshape(pair_count) - side * n_half
    expert_hits = (local_ids[:, None] == jnp.arange(n_half, dtype=jnp.int32)[None, :]).astype(
        jnp.int32
    )
    earlier = jnp.cumsum(expert_hits, axis=0) - expert_hits
    slot_index = jnp.sum(earlier * expert_hits, axis=1)
    in_half = jnp.sum(expert_hits, axis=1) > 0
    target = jnp.where(in_half, local_ids * capacity + slot_index, -1)
    placement = (
        jnp.arange(n_half * capacity, dtype=jnp.int32)[:, None] == target[None, :]
    ).astype(jnp.bfloat16)
    token_place = jnp.sum(placement.reshape(n_half, capacity, held, chosen_count), axis=3)
    outgoing = jnp.einsum(
        "hcp,pd->hcd", token_place, rows, preferred_element_type=jnp.float32
    ).astype(jnp.bfloat16)
    received = lax.all_to_all(outgoing, HALF, split_axis=0, concat_axis=0, tiled=True)
    gate_part = jnp.einsum("hcd,df->hcf", received, w_gate[0], preferred_element_type=jnp.float32)
    up_part = jnp.einsum("hcd,df->hcf", received, w_up[0], preferred_element_type=jnp.float32)
    activation = (jax.nn.silu(gate_part) * up_part).astype(jnp.bfloat16)
    activation = lax.optimization_barrier(activation)
    result = jnp.einsum(
        "hcf,fd->hcd", activation, w_down[0], preferred_element_type=jnp.float32
    ).astype(jnp.bfloat16)
    returned = lax.all_to_all(result, HALF, split_axis=0, concat_axis=0, tiled=True)
    pair_rows = jnp.einsum(
        "hcp,hcd->pd",
        placement.reshape(n_half, capacity, pair_count),
        returned,
        preferred_element_type=jnp.float32,
    )
    weighted = weights[..., None] * pair_rows.reshape(held, chosen_count, width)
    partial = jnp.sum(weighted, axis=1)
    mine = jnp.where(first, partial[:tok_here], partial[tok_here:])
    theirs = jnp.where(first, partial[tok_here:], partial[:tok_here])
    sent = swap_halves(theirs.astype(jnp.bfloat16)).astype(jnp.float32)
    return (mine + sent).astype(jnp.bfloat16)


def shards(
    query,
    new_key,
    new_value,
    cache_key,
    cache_value,
    lengths,
    hidden_in,
    out_weight,
    norm_gain,
    route_ids,
    route_weight,
    w_gate,
    w_up,
    w_down,
):
    heads_out = attend_local(query, new_key, new_value, cache_key, cache_value, lengths)
    n_dl = lax.axis_size("dl")
    n_t = lax.axis_size("tensor")
    tok_here = hidden_in.shape[0]
    first = lax.axis_index("zh") == 0
    other_heads = swap_halves(heads_out)
    pair_heads = jnp.where(
        first,
        jnp.concatenate([heads_out, other_heads]),
        jnp.concatenate([other_heads, heads_out]),
    )
    spread = jnp.broadcast_to(pair_heads[None], (n_dl,) + pair_heads.shape)
    gathered = lax.all_to_all(spread, "dl", split_axis=0, concat_axis=0, tiled=True)
    partial_cols = jnp.einsum(
        "sqd,df->sqf", gathered, out_weight, preferred_element_type=jnp.float32
    )
    col_width = partial_cols.shape[-1]
    by_dest = partial_cols.reshape(n_dl, 2, n_t, tok_here, col_width).transpose(1, 0, 2, 3, 4)
    by_dest = by_dest.reshape(2 * n_dl * n_t, tok_here, col_width)
    arrived = lax.all_to_all(
        by_dest.astype(jnp.bfloat16), DP + ("tensor",), split_axis=0, concat_axis=0, tiled=True
    )
    arrived = arrived.astype(jnp.float32).reshape(2 * n_dl, n_t, tok_here, col_width)
    summed = jnp.sum(arrived, axis=1)
    summed = summed.transpose(1, 0, 2).reshape(tok_here, 2 * n_dl * col_width)
    attended = (hidden_in.astype(jnp.float32) + summed).astype(jnp.bfloat16)
    widened = attended.astype(jnp.float32)
    scaled = widened * lax.rsqrt(jnp.mean(widened * widened, axis=-1, keepdims=True) + 1e-06)
    normed = (scaled * norm_gain).astype(jnp.bfloat16)
    expert_mix = expert_layer(normed, route_ids, route_weight, w_gate, w_up, w_down)
    return (attended, expert_mix)


def solution(mesh):
    n_dp = mesh.shape["dp"]
    devices = np.asarray(mesh.devices).reshape(2, n_dp // 2, mesh.shape["tensor"])
    split_mesh = Mesh(devices, ("zh", "dl", "tensor"))
    rows = DP + ("tensor",)
    in_specs = (
        P(DP, "tensor"),
        P(DP, "tensor"),
        P(DP, "tensor"),
        P(DP, None, "tensor"),
        P(DP, None, "tensor"),
        P(DP),
        P(rows, None),
        P("tensor", DP),
        P(),
        P(rows, None),
        P(rows, None),
        P(rows, None, None),
        P(rows, None, None),
        P(rows, None, None),
    )
    out_specs = (P(rows, None), P(rows, None))
    return jax.shard_map(
        shards, mesh=split_mesh, in_specs=in_specs, out_specs=out_specs, check_vma=False
    )
```

```python
import math

import jax
import jax.numpy as jnp
import numpy as np
from jax import lax
from jax.sharding import Mesh
from jax.sharding import PartitionSpec as P

HD = 128
DP = ("zh", "dl")
HALF = ("dl", "tensor")


def attend_local(query, new_key, new_value, cache_key, cache_value, lengths):
    row_count = query.shape[0]
    cache_len = cache_key.shape[1]
    kv_here = new_key.shape[1] // HD
    grouping = query.shape[1] // (kv_here * HD)
    queries = query.reshape(row_count, kv_here, grouping, HD)
    cache_keys = cache_key.reshape(row_count, cache_len, kv_here, HD)
    values = cache_value.reshape(row_count, cache_len, kv_here, HD)
    own_key = new_key.reshape(row_count, kv_here, HD)
    own_value = new_value.reshape(row_count, kv_here, HD)
    factor = 1.0 / math.sqrt(HD)
    scores = (
        jnp.einsum("rkgd,rckd->rkgc", queries, cache_keys, preferred_element_type=jnp.float32)
        * factor
    )
    own_score = (
        jnp.einsum("rkgd,rkd->rkg", queries, own_key, preferred_element_type=jnp.float32) * factor
    )
    visible = (jnp.arange(cache_len, dtype=jnp.int32)[None, :] < lengths[:, None])[:, None, None, :]
    highest = jnp.maximum(jnp.max(jnp.where(visible, scores, -1e30), axis=-1), own_score)
    exponent = jnp.where(visible, jnp.exp(scores - highest[..., None]), 0.0)
    own_exponent = jnp.exp(own_score - highest)
    totals = jnp.sum(exponent, axis=-1) + own_exponent
    probability = (exponent / totals[..., None]).astype(jnp.bfloat16)
    own_probability = (own_exponent / totals).astype(jnp.bfloat16)
    combined = jnp.einsum(
        "rkgc,rckd->rkgd", probability, values, preferred_element_type=jnp.float32
    )
    combined = (
        combined
        + own_probability.astype(jnp.float32)[..., None]
        * own_value.astype(jnp.float32)[:, :, None, :]
    )
    return combined.reshape(row_count, kv_here * grouping * HD).astype(jnp.bfloat16)


def swap_halves(x):
    return lax.ppermute(x, "zh", [(0, 1), (1, 0)])


def expert_layer(normed, route_ids, route_weight, w_gate, w_up, w_down):
    tok_here, width = normed.shape
    chosen_count = route_ids.shape[1]
    n_half = lax.axis_size("dl") * lax.axis_size("tensor")
    experts_all = 2 * n_half
    capacity = 2 * max(2, 3 * tok_here * chosen_count // experts_all)
    capacity = -(-capacity // 8) * 8
    side = lax.axis_index("zh")
    other_rows = swap_halves(normed)
    packed = swap_halves(jnp.concatenate([route_ids.astype(jnp.float32), route_weight], axis=1))
    other_ids = packed[:, :chosen_count].astype(jnp.int32)
    other_weight = packed[:, chosen_count:]
    first = side == 0
    rows = jnp.where(first, jnp.concatenate([normed, other_rows]), jnp.concatenate([other_rows, normed]))
    ids = jnp.where(first, jnp.concatenate([route_ids, other_ids]), jnp.concatenate([other_ids, route_ids]))
    weights = jnp.where(
        first,
        jnp.concatenate([route_weight, other_weight]),
        jnp.concatenate([other_weight, route_weight]),
    )
    held = 2 * tok_here
    pair_count = held * chosen_count
    local_ids = ids.reshape(pair_count) - side * n_half
    expert_hits = (local_ids[:, None] == jnp.arange(n_half, dtype=jnp.int32)[None, :]).astype(
        jnp.int32
    )
    earlier = jnp.cumsum(expert_hits, axis=0) - expert_hits
    slot_index = jnp.sum(earlier * expert_hits, axis=1)
    in_half = jnp.sum(expert_hits, axis=1) > 0
    target = jnp.where(in_half, local_ids * capacity + slot_index, -1)
    placement = (
        jnp.arange(n_half * capacity, dtype=jnp.int32)[:, None] == target[None, :]
    ).astype(jnp.bfloat16)
    token_place = jnp.sum(placement.reshape(n_half, capacity, held, chosen_count), axis=3)
    outgoing = jnp.einsum(
        "hcp,pd->hcd", token_place, rows, preferred_element_type=jnp.float32
    ).astype(jnp.bfloat16)
    received = lax.all_to_all(outgoing, HALF, split_axis=0, concat_axis=0, tiled=True)
    gate_part = jnp.einsum("hcd,df->hcf", received, w_gate[0], preferred_element_type=jnp.float32)
    up_part = jnp.einsum("hcd,df->hcf", received, w_up[0], preferred_element_type=jnp.float32)
    activation = (jax.nn.silu(gate_part) * up_part).astype(jnp.bfloat16)
    activation = lax.optimization_barrier(activation)
    result = jnp.einsum(
        "hcf,fd->hcd", activation, w_down[0], preferred_element_type=jnp.float32
    ).astype(jnp.bfloat16)
    returned = lax.all_to_all(result, HALF, split_axis=0, concat_axis=0, tiled=True)
    pair_rows = jnp.einsum(
        "hcp,hcd->pd",
        placement.reshape(n_half, capacity, pair_count),
        returned,
        preferred_element_type=jnp.float32,
    )
    weighted = weights[..., None] * pair_rows.reshape(held, chosen_count, width)
    partial = jnp.sum(weighted, axis=1)
    mine = jnp.where(first, partial[:tok_here], partial[tok_here:])
    theirs = jnp.where(first, partial[tok_here:], partial[:tok_here])
    sent = swap_halves(theirs.astype(jnp.bfloat16)).astype(jnp.float32)
    return (mine + sent).astype(jnp.bfloat16)


def shards(
    query,
    new_key,
    new_value,
    cache_key,
    cache_value,
    lengths,
    hidden_in,
    out_weight,
    norm_gain,
    route_ids,
    route_weight,
    w_gate,
    w_up,
    w_down,
):
    heads_out = attend_local(query, new_key, new_value, cache_key, cache_value, lengths)
    n_dl = lax.axis_size("dl")
    n_t = lax.axis_size("tensor")
    tok_here = hidden_in.shape[0]
    first = lax.axis_index("zh") == 0

    def project(block):
        spread = jnp.broadcast_to(block[None], (n_dl,) + block.shape)
        gathered = lax.all_to_all(spread, "dl", split_axis=0, concat_axis=0, tiled=True)
        return jnp.einsum("sqd,df->sqf", gathered, out_weight, preferred_element_type=jnp.float32)

    own_cols = project(heads_out)
    other_cols = project(swap_halves(heads_out))
    by_side = jnp.where(
        first, jnp.stack([own_cols, other_cols]), jnp.stack([other_cols, own_cols])
    )
    col_width = by_side.shape[-1]
    by_dest = by_side.reshape(2 * n_dl * n_t, tok_here, col_width)
    arrived = lax.all_to_all(
        by_dest.astype(jnp.bfloat16), DP + ("tensor",), split_axis=0, concat_axis=0, tiled=True
    )
    arrived = arrived.astype(jnp.float32).reshape(2 * n_dl, n_t, tok_here, col_width)
    summed = jnp.sum(arrived, axis=1)
    summed = summed.transpose(1, 0, 2).reshape(tok_here, 2 * n_dl * col_width)
    attended = (hidden_in.astype(jnp.float32) + summed).astype(jnp.bfloat16)
    widened = attended.astype(jnp.float32)
    scaled = widened * lax.rsqrt(jnp.mean(widened * widened, axis=-1, keepdims=True) + 1e-06)
    normed = (scaled * norm_gain).astype(jnp.bfloat16)
    expert_mix = expert_layer(normed, route_ids, route_weight, w_gate, w_up, w_down)
    return (attended, expert_mix)


def solution(mesh):
    n_dp = mesh.shape["dp"]
    devices = np.asarray(mesh.devices).reshape(2, n_dp // 2, mesh.shape["tensor"])
    split_mesh = Mesh(devices, ("zh", "dl", "tensor"))
    rows = DP + ("tensor",)
    in_specs = (
        P(DP, "tensor"),
        P(DP, "tensor"),
        P(DP, "tensor"),
        P(DP, None, "tensor"),
        P(DP, None, "tensor"),
        P(DP),
        P(rows, None),
        P("tensor", DP),
        P(),
        P(rows, None),
        P(rows, None),
        P(rows, None, None),
        P(rows, None, None),
        P(rows, None, None),
    )
    out_specs = (P(rows, None), P(rows, None))
    return jax.shard_map(
        shards, mesh=split_mesh, in_specs=in_specs, out_specs=out_specs, check_vma=False
    )
```

```python
import math

import jax
import jax.numpy as jnp
import numpy as np
from jax import lax
from jax.sharding import Mesh
from jax.sharding import PartitionSpec as P

HD = 128
DP = ("zh", "dl")
HALF = ("dl", "tensor")


def attend_local(query, new_key, new_value, cache_key, cache_value, lengths):
    row_count = query.shape[0]
    cache_len = cache_key.shape[1]
    kv_here = new_key.shape[1] // HD
    grouping = query.shape[1] // (kv_here * HD)
    queries = query.reshape(row_count, kv_here, grouping, HD)
    cache_keys = cache_key.reshape(row_count, cache_len, kv_here, HD)
    values = cache_value.reshape(row_count, cache_len, kv_here, HD)
    own_key = new_key.reshape(row_count, kv_here, HD)
    own_value = new_value.reshape(row_count, kv_here, HD)
    factor = 1.0 / math.sqrt(HD)
    scores = (
        jnp.einsum("rkgd,rckd->rkgc", queries, cache_keys, preferred_element_type=jnp.float32)
        * factor
    )
    own_score = (
        jnp.einsum("rkgd,rkd->rkg", queries, own_key, preferred_element_type=jnp.float32) * factor
    )
    visible = (jnp.arange(cache_len, dtype=jnp.int32)[None, :] < lengths[:, None])[:, None, None, :]
    highest = jnp.maximum(jnp.max(jnp.where(visible, scores, -1e30), axis=-1), own_score)
    exponent = jnp.where(visible, jnp.exp(scores - highest[..., None]), 0.0)
    own_exponent = jnp.exp(own_score - highest)
    totals = jnp.sum(exponent, axis=-1) + own_exponent
    probability = (exponent / totals[..., None]).astype(jnp.bfloat16)
    own_probability = (own_exponent / totals).astype(jnp.bfloat16)
    combined = jnp.einsum(
        "rkgc,rckd->rkgd", probability, values, preferred_element_type=jnp.float32
    )
    combined = (
        combined
        + own_probability.astype(jnp.float32)[..., None]
        * own_value.astype(jnp.float32)[:, :, None, :]
    )
    return combined.reshape(row_count, kv_here * grouping * HD).astype(jnp.bfloat16)


def swap_halves(x):
    return lax.ppermute(x, "zh", [(0, 1), (1, 0)])


def expert_layer(normed, route_ids, route_weight, w_gate, w_up, w_down):
    tok_here, width = normed.shape
    chosen_count = route_ids.shape[1]
    n_half = lax.axis_size("dl") * lax.axis_size("tensor")
    experts_all = 2 * n_half
    capacity = 2 * max(2, 3 * tok_here * chosen_count // experts_all)
    capacity = -(-capacity // 8) * 8
    side = lax.axis_index("zh")
    other_rows = swap_halves(normed)
    packed = swap_halves(jnp.concatenate([route_ids.astype(jnp.float32), route_weight], axis=1))
    other_ids = packed[:, :chosen_count].astype(jnp.int32)
    other_weight = packed[:, chosen_count:]
    rows = jnp.concatenate([normed, other_rows])
    ids = jnp.concatenate([route_ids, other_ids])
    held = 2 * tok_here
    pair_count = held * chosen_count
    local_ids = ids.reshape(pair_count) - side * n_half
    expert_hits = (local_ids[:, None] == jnp.arange(n_half, dtype=jnp.int32)[None, :]).astype(
        jnp.int32
    )
    earlier = jnp.cumsum(expert_hits, axis=0) - expert_hits
    slot_index = jnp.sum(earlier * expert_hits, axis=1)
    in_half = jnp.sum(expert_hits, axis=1) > 0
    target = jnp.where(in_half, local_ids * capacity + slot_index, -1)
    placement = (
        jnp.arange(n_half * capacity, dtype=jnp.int32)[:, None] == target[None, :]
    ).astype(jnp.bfloat16)
    token_place = jnp.sum(placement.reshape(n_half, capacity, held, chosen_count), axis=3)
    outgoing = jnp.einsum(
        "hcp,pd->hcd", token_place, rows, preferred_element_type=jnp.float32
    ).astype(jnp.bfloat16)
    received = lax.all_to_all(outgoing, HALF, split_axis=0, concat_axis=0, tiled=True)
    gate_part = jnp.einsum("hcd,df->hcf", received, w_gate[0], preferred_element_type=jnp.float32)
    up_part = jnp.einsum("hcd,df->hcf", received, w_up[0], preferred_element_type=jnp.float32)
    activation = (jax.nn.silu(gate_part) * up_part).astype(jnp.bfloat16)
    activation = lax.optimization_barrier(activation)
    result = jnp.einsum(
        "hcf,fd->hcd", activation, w_down[0], preferred_element_type=jnp.float32
    ).astype(jnp.bfloat16)
    returned = lax.all_to_all(result, HALF, split_axis=0, concat_axis=0, tiled=True)
    placement = placement.reshape(n_half, capacity, 2, tok_here * chosen_count)

    def combine(block, weight):
        pair_rows = jnp.einsum(
            "hcp,hcd->pd", placement[:, :, block], returned, preferred_element_type=jnp.float32
        )
        weighted = weight[..., None] * pair_rows.reshape(tok_here, chosen_count, width)
        return jnp.sum(weighted, axis=1)

    sent = swap_halves(combine(1, other_weight).astype(jnp.bfloat16)).astype(jnp.float32)
    return (combine(0, route_weight) + sent).astype(jnp.bfloat16)


def shards(
    query,
    new_key,
    new_value,
    cache_key,
    cache_value,
    lengths,
    hidden_in,
    out_weight,
    norm_gain,
    route_ids,
    route_weight,
    w_gate,
    w_up,
    w_down,
):
    heads_out = attend_local(query, new_key, new_value, cache_key, cache_value, lengths)
    n_dl = lax.axis_size("dl")
    n_t = lax.axis_size("tensor")
    tok_here = hidden_in.shape[0]
    first = lax.axis_index("zh") == 0

    def project(block):
        spread = jnp.broadcast_to(block[None], (n_dl,) + block.shape)
        gathered = lax.all_to_all(spread, "dl", split_axis=0, concat_axis=0, tiled=True)
        return jnp.einsum("sqd,df->sqf", gathered, out_weight, preferred_element_type=jnp.float32)

    own_cols = project(heads_out)
    other_cols = project(swap_halves(heads_out))
    by_side = jnp.where(
        first, jnp.stack([own_cols, other_cols]), jnp.stack([other_cols, own_cols])
    )
    col_width = by_side.shape[-1]
    by_dest = by_side.reshape(2 * n_dl * n_t, tok_here, col_width)
    arrived = lax.all_to_all(
        by_dest.astype(jnp.bfloat16), DP + ("tensor",), split_axis=0, concat_axis=0, tiled=True
    )
    arrived = arrived.astype(jnp.float32).reshape(2 * n_dl, n_t, tok_here, col_width)
    summed = jnp.sum(arrived, axis=1)
    summed = summed.transpose(1, 0, 2).reshape(tok_here, 2 * n_dl * col_width)
    attended = (hidden_in.astype(jnp.float32) + summed).astype(jnp.bfloat16)
    widened = attended.astype(jnp.float32)
    scaled = widened * lax.rsqrt(jnp.mean(widened * widened, axis=-1, keepdims=True) + 1e-06)
    normed = (scaled * norm_gain).astype(jnp.bfloat16)
    expert_mix = expert_layer(normed, route_ids, route_weight, w_gate, w_up, w_down)
    return (attended, expert_mix)


def solution(mesh):
    n_dp = mesh.shape["dp"]
    devices = np.asarray(mesh.devices).reshape(2, n_dp // 2, mesh.shape["tensor"])
    split_mesh = Mesh(devices, ("zh", "dl", "tensor"))
    rows = DP + ("tensor",)
    in_specs = (
        P(DP, "tensor"),
        P(DP, "tensor"),
        P(DP, "tensor"),
        P(DP, None, "tensor"),
        P(DP, None, "tensor"),
        P(DP),
        P(rows, None),
        P("tensor", DP),
        P(),
        P(rows, None),
        P(rows, None),
        P(rows, None, None),
        P(rows, None, None),
        P(rows, None, None),
    )
    out_specs = (P(rows, None), P(rows, None))
    return jax.shard_map(
        shards, mesh=split_mesh, in_specs=in_specs, out_specs=out_specs, check_vma=False
    )
```

```python
import math

import jax
import jax.numpy as jnp
import numpy as np
from jax import lax
from jax.sharding import Mesh
from jax.sharding import PartitionSpec as P

HD = 128
DP = ("zh", "dl")
HALF = ("dl", "tensor")


def attend_local(query, new_key, new_value, cache_key, cache_value, lengths):
    row_count = query.shape[0]
    cache_len = cache_key.shape[1]
    kv_here = new_key.shape[1] // HD
    grouping = query.shape[1] // (kv_here * HD)
    queries = query.reshape(row_count, kv_here, grouping, HD)
    cache_keys = cache_key.reshape(row_count, cache_len, kv_here, HD)
    values = cache_value.reshape(row_count, cache_len, kv_here, HD)
    own_key = new_key.reshape(row_count, kv_here, HD)
    own_value = new_value.reshape(row_count, kv_here, HD)
    factor = 1.0 / math.sqrt(HD)
    scores = (
        jnp.einsum("rkgd,rckd->rkgc", queries, cache_keys, preferred_element_type=jnp.float32)
        * factor
    )
    own_score = (
        jnp.einsum("rkgd,rkd->rkg", queries, own_key, preferred_element_type=jnp.float32) * factor
    )
    visible = (jnp.arange(cache_len, dtype=jnp.int32)[None, :] < lengths[:, None])[:, None, None, :]
    highest = jnp.maximum(jnp.max(jnp.where(visible, scores, -1e30), axis=-1), own_score)
    exponent = jnp.where(visible, jnp.exp(scores - highest[..., None]), 0.0)
    own_exponent = jnp.exp(own_score - highest)
    totals = jnp.sum(exponent, axis=-1) + own_exponent
    probability = (exponent / totals[..., None]).astype(jnp.bfloat16)
    own_probability = (own_exponent / totals).astype(jnp.bfloat16)
    combined = jnp.einsum(
        "rkgc,rckd->rkgd", probability, values, preferred_element_type=jnp.float32
    )
    combined = (
        combined
        + own_probability.astype(jnp.float32)[..., None]
        * own_value.astype(jnp.float32)[:, :, None, :]
    )
    return combined.reshape(row_count, kv_here * grouping * HD).astype(jnp.bfloat16)


def swap_halves(x):
    return lax.ppermute(x, "zh", [(0, 1), (1, 0)])


def expert_layer(normed, route_ids, route_weight, w_gate, w_up, w_down):
    tok_here, width = normed.shape
    chosen_count = route_ids.shape[1]
    n_half = lax.axis_size("dl") * lax.axis_size("tensor")
    experts_all = 2 * n_half
    capacity = 2 * max(2, 3 * tok_here * chosen_count // experts_all)
    capacity = -(-capacity // 8) * 8
    side = lax.axis_index("zh")
    other_rows = swap_halves(normed)
    packed = swap_halves(jnp.concatenate([route_ids.astype(jnp.float32), route_weight], axis=1))
    other_ids = packed[:, :chosen_count].astype(jnp.int32)
    other_weight = packed[:, chosen_count:]
    rows = jnp.concatenate([normed, other_rows])
    ids = jnp.concatenate([route_ids, other_ids])
    held = 2 * tok_here
    pair_count = held * chosen_count
    local_ids = ids.reshape(pair_count) - side * n_half
    expert_hits = (local_ids[:, None] == jnp.arange(n_half, dtype=jnp.int32)[None, :]).astype(
        jnp.int32
    )
    earlier = jnp.cumsum(expert_hits, axis=0) - expert_hits
    slot_index = jnp.sum(earlier * expert_hits, axis=1)
    in_half = jnp.sum(expert_hits, axis=1) > 0
    target = jnp.where(in_half, local_ids * capacity + slot_index, -1)
    placement = (
        jnp.arange(n_half * capacity, dtype=jnp.int32)[:, None] == target[None, :]
    ).astype(jnp.bfloat16)
    token_place = jnp.sum(placement.reshape(n_half, capacity, held, chosen_count), axis=3)
    outgoing = jnp.einsum(
        "hcp,pd->hcd", token_place, rows, preferred_element_type=jnp.float32
    ).astype(jnp.bfloat16)
    received = lax.all_to_all(outgoing, HALF, split_axis=0, concat_axis=0, tiled=True)
    gate_part = jnp.einsum("hcd,df->hcf", received, w_gate[0], preferred_element_type=jnp.float32)
    up_part = jnp.einsum("hcd,df->hcf", received, w_up[0], preferred_element_type=jnp.float32)
    activation = (jax.nn.silu(gate_part) * up_part).astype(jnp.bfloat16)
    activation = lax.optimization_barrier(activation)
    result = jnp.einsum(
        "hcf,fd->hcd", activation, w_down[0], preferred_element_type=jnp.float32
    ).astype(jnp.bfloat16)
    lanes = 128
    used = min(capacity, 2 * max(2, 3 * tok_here * chosen_count // experts_all))
    back = result[:, :used].reshape(n_half, used * (width // lanes), lanes)
    returned = lax.all_to_all(back, HALF, split_axis=0, concat_axis=0, tiled=True)
    returned = returned.reshape(n_half, used, width // lanes, lanes)
    placement = placement.reshape(n_half, capacity, 2, tok_here * chosen_count)[:, :used]

    def combine(block, weight):
        pair_rows = jnp.einsum(
            "hcp,hcql->pql", placement[:, :, block], returned, preferred_element_type=jnp.float32
        ).reshape(tok_here * chosen_count, width)
        weighted = weight[..., None] * pair_rows.reshape(tok_here, chosen_count, width)
        return jnp.sum(weighted, axis=1)

    sent = swap_halves(combine(1, other_weight).astype(jnp.bfloat16)).astype(jnp.float32)
    return (combine(0, route_weight) + sent).astype(jnp.bfloat16)


def shards(
    query,
    new_key,
    new_value,
    cache_key,
    cache_value,
    lengths,
    hidden_in,
    out_weight,
    norm_gain,
    route_ids,
    route_weight,
    w_gate,
    w_up,
    w_down,
):
    heads_out = attend_local(query, new_key, new_value, cache_key, cache_value, lengths)
    n_dl = lax.axis_size("dl")
    n_t = lax.axis_size("tensor")
    tok_here = hidden_in.shape[0]
    first = lax.axis_index("zh") == 0

    def project(block):
        spread = jnp.broadcast_to(block[None], (n_dl,) + block.shape)
        gathered = lax.all_to_all(spread, "dl", split_axis=0, concat_axis=0, tiled=True)
        return jnp.einsum("sqd,df->sqf", gathered, out_weight, preferred_element_type=jnp.float32)

    own_cols = project(heads_out)
    other_cols = project(swap_halves(heads_out))
    by_side = jnp.where(
        first, jnp.stack([own_cols, other_cols]), jnp.stack([other_cols, own_cols])
    )
    col_width = by_side.shape[-1]
    by_dest = by_side.reshape(2 * n_dl * n_t, tok_here, col_width)
    arrived = lax.all_to_all(
        by_dest.astype(jnp.bfloat16), DP + ("tensor",), split_axis=0, concat_axis=0, tiled=True
    )
    arrived = arrived.astype(jnp.float32).reshape(2 * n_dl, n_t, tok_here, col_width)
    summed = jnp.sum(arrived, axis=1)
    summed = summed.transpose(1, 0, 2).reshape(tok_here, 2 * n_dl * col_width)
    attended = (hidden_in.astype(jnp.float32) + summed).astype(jnp.bfloat16)
    widened = attended.astype(jnp.float32)
    scaled = widened * lax.rsqrt(jnp.mean(widened * widened, axis=-1, keepdims=True) + 1e-06)
    normed = (scaled * norm_gain).astype(jnp.bfloat16)
    expert_mix = expert_layer(normed, route_ids, route_weight, w_gate, w_up, w_down)
    return (attended, expert_mix)


def solution(mesh):
    n_dp = mesh.shape["dp"]
    devices = np.asarray(mesh.devices).reshape(2, n_dp // 2, mesh.shape["tensor"])
    split_mesh = Mesh(devices, ("zh", "dl", "tensor"))
    rows = DP + ("tensor",)
    in_specs = (
        P(DP, "tensor"),
        P(DP, "tensor"),
        P(DP, "tensor"),
        P(DP, None, "tensor"),
        P(DP, None, "tensor"),
        P(DP),
        P(rows, None),
        P("tensor", DP),
        P(),
        P(rows, None),
        P(rows, None),
        P(rows, None, None),
        P(rows, None, None),
        P(rows, None, None),
    )
    out_specs = (P(rows, None), P(rows, None))
    return jax.shard_map(
        shards, mesh=split_mesh, in_specs=in_specs, out_specs=out_specs, check_vma=False
    )
```

```python
import math

import jax
import jax.numpy as jnp
import numpy as np
from jax import lax
from jax.sharding import Mesh
from jax.sharding import PartitionSpec as P

HD = 128
DP = ("zh", "dl")
HALF = ("dl", "tensor")


def attend_local(query, new_key, new_value, cache_key, cache_value, lengths):
    row_count = query.shape[0]
    cache_len = cache_key.shape[1]
    kv_here = new_key.shape[1] // HD
    grouping = query.shape[1] // (kv_here * HD)
    queries = query.reshape(row_count, kv_here, grouping, HD)
    cache_keys = cache_key.reshape(row_count, cache_len, kv_here, HD)
    values = cache_value.reshape(row_count, cache_len, kv_here, HD)
    own_key = new_key.reshape(row_count, kv_here, HD)
    own_value = new_value.reshape(row_count, kv_here, HD)
    factor = 1.0 / math.sqrt(HD)
    scores = (
        jnp.einsum("rkgd,rckd->rkgc", queries, cache_keys, preferred_element_type=jnp.float32)
        * factor
    )
    own_score = (
        jnp.einsum("rkgd,rkd->rkg", queries, own_key, preferred_element_type=jnp.float32) * factor
    )
    visible = (jnp.arange(cache_len, dtype=jnp.int32)[None, :] < lengths[:, None])[:, None, None, :]
    highest = jnp.maximum(jnp.max(jnp.where(visible, scores, -1e30), axis=-1), own_score)
    exponent = jnp.where(visible, jnp.exp(scores - highest[..., None]), 0.0)
    own_exponent = jnp.exp(own_score - highest)
    totals = jnp.sum(exponent, axis=-1) + own_exponent
    probability = (exponent / totals[..., None]).astype(jnp.bfloat16)
    own_probability = (own_exponent / totals).astype(jnp.bfloat16)
    combined = jnp.einsum(
        "rkgc,rckd->rkgd", probability, values, preferred_element_type=jnp.float32
    )
    combined = (
        combined
        + own_probability.astype(jnp.float32)[..., None]
        * own_value.astype(jnp.float32)[:, :, None, :]
    )
    return combined.reshape(row_count, kv_here * grouping * HD).astype(jnp.bfloat16)


def swap_halves(x):
    return lax.ppermute(x, "zh", [(0, 1), (1, 0)])


def expert_layer(normed, route_ids, route_weight, w_gate, w_up, w_down):
    tok_here, width = normed.shape
    chosen_count = route_ids.shape[1]
    n_half = lax.axis_size("dl") * lax.axis_size("tensor")
    experts_all = 2 * n_half
    capacity = 2 * max(2, 3 * tok_here * chosen_count // experts_all)
    capacity = -(-capacity // 8) * 8
    side = lax.axis_index("zh")
    other_rows = swap_halves(normed)
    packed = swap_halves(jnp.concatenate([route_ids.astype(jnp.float32), route_weight], axis=1))
    other_ids = packed[:, :chosen_count].astype(jnp.int32)
    other_weight = packed[:, chosen_count:]
    rows = jnp.concatenate([normed, other_rows])
    ids = jnp.concatenate([route_ids, other_ids])
    held = 2 * tok_here
    pair_count = held * chosen_count
    local_ids = ids.reshape(pair_count) - side * n_half
    expert_hits = (local_ids[:, None] == jnp.arange(n_half, dtype=jnp.int32)[None, :]).astype(
        jnp.int32
    )
    earlier = jnp.cumsum(expert_hits, axis=0) - expert_hits
    slot_index = jnp.sum(earlier * expert_hits, axis=1)
    in_half = jnp.sum(expert_hits, axis=1) > 0
    target = jnp.where(in_half, local_ids * capacity + slot_index, -1)
    placement = (
        jnp.arange(n_half * capacity, dtype=jnp.int32)[:, None] == target[None, :]
    ).astype(jnp.bfloat16)
    token_place = jnp.sum(placement.reshape(n_half, capacity, held, chosen_count), axis=3)
    outgoing = jnp.einsum(
        "hcp,pd->hcd", token_place, rows, preferred_element_type=jnp.float32
    ).astype(jnp.bfloat16)
    received = lax.all_to_all(outgoing, HALF, split_axis=0, concat_axis=0, tiled=True)
    gate_part = jnp.einsum("hcd,df->hcf", received, w_gate[0], preferred_element_type=jnp.float32)
    up_part = jnp.einsum("hcd,df->hcf", received, w_up[0], preferred_element_type=jnp.float32)
    activation = (jax.nn.silu(gate_part) * up_part).astype(jnp.bfloat16)
    activation = lax.optimization_barrier(activation)
    result = jnp.einsum(
        "hcf,fd->hcd", activation, w_down[0], preferred_element_type=jnp.float32
    ).astype(jnp.bfloat16)
    lanes = 128
    used = min(capacity, 2 * max(2, 3 * tok_here * chosen_count // experts_all))
    back = result[:, :used].reshape(n_half, used * (width // lanes), lanes)
    returned = lax.all_to_all(back, HALF, split_axis=0, concat_axis=0, tiled=True)
    returned = returned.reshape(n_half * used, width)
    placement = placement.reshape(n_half, capacity, 2, tok_here * chosen_count)[:, :used]
    placement = placement.reshape(n_half * used, 2, tok_here * chosen_count)

    def combine(block, weight):
        pair_rows = jnp.einsum(
            "sp,sd->pd", placement[:, block], returned, preferred_element_type=jnp.float32
        )
        weighted = weight[..., None] * pair_rows.reshape(tok_here, chosen_count, width)
        return jnp.sum(weighted, axis=1)

    sent = swap_halves(combine(1, other_weight).astype(jnp.bfloat16)).astype(jnp.float32)
    return (combine(0, route_weight) + sent).astype(jnp.bfloat16)


def shards(
    query,
    new_key,
    new_value,
    cache_key,
    cache_value,
    lengths,
    hidden_in,
    out_weight,
    norm_gain,
    route_ids,
    route_weight,
    w_gate,
    w_up,
    w_down,
):
    heads_out = attend_local(query, new_key, new_value, cache_key, cache_value, lengths)
    n_dl = lax.axis_size("dl")
    n_t = lax.axis_size("tensor")
    tok_here = hidden_in.shape[0]
    first = lax.axis_index("zh") == 0

    def project(block):
        spread = jnp.broadcast_to(block[None], (n_dl,) + block.shape)
        gathered = lax.all_to_all(spread, "dl", split_axis=0, concat_axis=0, tiled=True)
        return jnp.einsum("sqd,df->sqf", gathered, out_weight, preferred_element_type=jnp.float32)

    own_cols = project(heads_out)
    other_cols = project(swap_halves(heads_out))
    by_side = jnp.where(
        first, jnp.stack([own_cols, other_cols]), jnp.stack([other_cols, own_cols])
    )
    col_width = by_side.shape[-1]
    by_dest = by_side.reshape(2 * n_dl * n_t, tok_here, col_width)
    arrived = lax.all_to_all(
        by_dest.astype(jnp.bfloat16), DP + ("tensor",), split_axis=0, concat_axis=0, tiled=True
    )
    arrived = arrived.astype(jnp.float32).reshape(2 * n_dl, n_t, tok_here, col_width)
    summed = jnp.sum(arrived, axis=1)
    summed = summed.transpose(1, 0, 2).reshape(tok_here, 2 * n_dl * col_width)
    attended = (hidden_in.astype(jnp.float32) + summed).astype(jnp.bfloat16)
    widened = attended.astype(jnp.float32)
    scaled = widened * lax.rsqrt(jnp.mean(widened * widened, axis=-1, keepdims=True) + 1e-06)
    normed = (scaled * norm_gain).astype(jnp.bfloat16)
    expert_mix = expert_layer(normed, route_ids, route_weight, w_gate, w_up, w_down)
    return (attended, expert_mix)


def solution(mesh):
    n_dp = mesh.shape["dp"]
    devices = np.asarray(mesh.devices).reshape(2, n_dp // 2, mesh.shape["tensor"])
    split_mesh = Mesh(devices, ("zh", "dl", "tensor"))
    rows = DP + ("tensor",)
    in_specs = (
        P(DP, "tensor"),
        P(DP, "tensor"),
        P(DP, "tensor"),
        P(DP, None, "tensor"),
        P(DP, None, "tensor"),
        P(DP),
        P(rows, None),
        P("tensor", DP),
        P(),
        P(rows, None),
        P(rows, None),
        P(rows, None, None),
        P(rows, None, None),
        P(rows, None, None),
    )
    out_specs = (P(rows, None), P(rows, None))
    return jax.shard_map(
        shards, mesh=split_mesh, in_specs=in_specs, out_specs=out_specs, check_vma=False
    )
```

```python
import math

import jax
import jax.numpy as jnp
import numpy as np
from jax import lax
from jax.sharding import Mesh
from jax.sharding import PartitionSpec as P

HD = 128
DP = ("zh", "dl")
HALF = ("dl", "tensor")


def attend_local(query, new_key, new_value, cache_key, cache_value, lengths):
    row_count = query.shape[0]
    cache_len = cache_key.shape[1]
    kv_here = new_key.shape[1] // HD
    grouping = query.shape[1] // (kv_here * HD)
    queries = query.reshape(row_count, kv_here, grouping, HD)
    cache_keys = cache_key.reshape(row_count, cache_len, kv_here, HD)
    values = cache_value.reshape(row_count, cache_len, kv_here, HD)
    own_key = new_key.reshape(row_count, kv_here, HD)
    own_value = new_value.reshape(row_count, kv_here, HD)
    factor = 1.0 / math.sqrt(HD)
    scores = (
        jnp.einsum("rkgd,rckd->rkgc", queries, cache_keys, preferred_element_type=jnp.float32)
        * factor
    )
    own_score = (
        jnp.einsum("rkgd,rkd->rkg", queries, own_key, preferred_element_type=jnp.float32) * factor
    )
    visible = (jnp.arange(cache_len, dtype=jnp.int32)[None, :] < lengths[:, None])[:, None, None, :]
    highest = jnp.maximum(jnp.max(jnp.where(visible, scores, -1e30), axis=-1), own_score)
    exponent = jnp.where(visible, jnp.exp(scores - highest[..., None]), 0.0)
    own_exponent = jnp.exp(own_score - highest)
    totals = jnp.sum(exponent, axis=-1) + own_exponent
    probability = (exponent / totals[..., None]).astype(jnp.bfloat16)
    own_probability = (own_exponent / totals).astype(jnp.bfloat16)
    combined = jnp.einsum(
        "rkgc,rckd->rkgd", probability, values, preferred_element_type=jnp.float32
    )
    combined = (
        combined
        + own_probability.astype(jnp.float32)[..., None]
        * own_value.astype(jnp.float32)[:, :, None, :]
    )
    return combined.reshape(row_count, kv_here * grouping * HD).astype(jnp.bfloat16)


def swap_halves(x):
    return lax.ppermute(x, "zh", [(0, 1), (1, 0)])


def expert_layer(normed, route_ids, route_weight, w_gate, w_up, w_down):
    tok_here, width = normed.shape
    chosen_count = route_ids.shape[1]
    n_half = lax.axis_size("dl") * lax.axis_size("tensor")
    experts_all = 2 * n_half
    capacity = 2 * max(2, 3 * tok_here * chosen_count // experts_all)
    side = lax.axis_index("zh")
    other_rows = swap_halves(normed)
    packed = swap_halves(jnp.concatenate([route_ids.astype(jnp.float32), route_weight], axis=1))
    other_ids = packed[:, :chosen_count].astype(jnp.int32)
    other_weight = packed[:, chosen_count:]
    rows = jnp.concatenate([normed, other_rows])
    ids = jnp.concatenate([route_ids, other_ids])
    held = 2 * tok_here
    pair_count = held * chosen_count
    local_ids = ids.reshape(pair_count) - side * n_half
    expert_hits = (local_ids[:, None] == jnp.arange(n_half, dtype=jnp.int32)[None, :]).astype(
        jnp.int32
    )
    earlier = jnp.cumsum(expert_hits, axis=0) - expert_hits
    slot_index = jnp.sum(earlier * expert_hits, axis=1)
    in_half = jnp.sum(expert_hits, axis=1) > 0
    target = jnp.where(in_half, local_ids * capacity + slot_index, -1)
    placement = (
        jnp.arange(n_half * capacity, dtype=jnp.int32)[:, None] == target[None, :]
    ).astype(jnp.bfloat16)
    token_place = jnp.sum(placement.reshape(n_half * capacity, held, chosen_count), axis=2)
    outgoing = jnp.dot(token_place, rows, preferred_element_type=jnp.float32).astype(jnp.bfloat16)
    lanes = 128
    packed_shape = (n_half, capacity * (width // lanes), lanes)
    received = lax.all_to_all(
        outgoing.reshape(packed_shape), HALF, split_axis=0, concat_axis=0, tiled=True
    )
    flat_rows = received.reshape(n_half * capacity, width)
    gate_part = jnp.dot(flat_rows, w_gate[0], preferred_element_type=jnp.float32)
    up_part = jnp.dot(flat_rows, w_up[0], preferred_element_type=jnp.float32)
    activation = (jax.nn.silu(gate_part) * up_part).astype(jnp.bfloat16)
    activation = lax.optimization_barrier(activation)
    result = jnp.dot(activation, w_down[0], preferred_element_type=jnp.float32).astype(jnp.bfloat16)
    returned = lax.all_to_all(
        result.reshape(packed_shape), HALF, split_axis=0, concat_axis=0, tiled=True
    )
    returned = returned.reshape(n_half * capacity, width)
    placement = placement.reshape(n_half * capacity, 2, tok_here * chosen_count)

    def combine(block, weight):
        pair_rows = jnp.einsum(
            "sp,sd->pd", placement[:, block], returned, preferred_element_type=jnp.float32
        )
        weighted = weight[..., None] * pair_rows.reshape(tok_here, chosen_count, width)
        return jnp.sum(weighted, axis=1)

    sent = swap_halves(combine(1, other_weight).astype(jnp.bfloat16)).astype(jnp.float32)
    return (combine(0, route_weight) + sent).astype(jnp.bfloat16)


def shards(
    query,
    new_key,
    new_value,
    cache_key,
    cache_value,
    lengths,
    hidden_in,
    out_weight,
    norm_gain,
    route_ids,
    route_weight,
    w_gate,
    w_up,
    w_down,
):
    heads_out = attend_local(query, new_key, new_value, cache_key, cache_value, lengths)
    n_dl = lax.axis_size("dl")
    n_t = lax.axis_size("tensor")
    tok_here = hidden_in.shape[0]
    first = lax.axis_index("zh") == 0

    def project(block):
        spread = jnp.broadcast_to(block[None], (n_dl,) + block.shape)
        gathered = lax.all_to_all(spread, "dl", split_axis=0, concat_axis=0, tiled=True)
        return jnp.einsum("sqd,df->sqf", gathered, out_weight, preferred_element_type=jnp.float32)

    own_cols = project(heads_out)
    other_cols = project(swap_halves(heads_out))
    by_side = jnp.where(
        first, jnp.stack([own_cols, other_cols]), jnp.stack([other_cols, own_cols])
    )
    col_width = by_side.shape[-1]
    by_dest = by_side.reshape(2 * n_dl * n_t, tok_here, col_width)
    arrived = lax.all_to_all(
        by_dest.astype(jnp.bfloat16), DP + ("tensor",), split_axis=0, concat_axis=0, tiled=True
    )
    arrived = arrived.astype(jnp.float32).reshape(2 * n_dl, n_t, tok_here, col_width)
    summed = jnp.sum(arrived, axis=1)
    summed = summed.transpose(1, 0, 2).reshape(tok_here, 2 * n_dl * col_width)
    attended = (hidden_in.astype(jnp.float32) + summed).astype(jnp.bfloat16)
    widened = attended.astype(jnp.float32)
    scaled = widened * lax.rsqrt(jnp.mean(widened * widened, axis=-1, keepdims=True) + 1e-06)
    normed = (scaled * norm_gain).astype(jnp.bfloat16)
    expert_mix = expert_layer(normed, route_ids, route_weight, w_gate, w_up, w_down)
    return (attended, expert_mix)


def solution(mesh):
    n_dp = mesh.shape["dp"]
    devices = np.asarray(mesh.devices).reshape(2, n_dp // 2, mesh.shape["tensor"])
    split_mesh = Mesh(devices, ("zh", "dl", "tensor"))
    rows = DP + ("tensor",)
    in_specs = (
        P(DP, "tensor"),
        P(DP, "tensor"),
        P(DP, "tensor"),
        P(DP, None, "tensor"),
        P(DP, None, "tensor"),
        P(DP),
        P(rows, None),
        P("tensor", DP),
        P(),
        P(rows, None),
        P(rows, None),
        P(rows, None, None),
        P(rows, None, None),
        P(rows, None, None),
    )
    out_specs = (P(rows, None), P(rows, None))
    return jax.shard_map(
        shards, mesh=split_mesh, in_specs=in_specs, out_specs=out_specs, check_vma=False
    )
```

```python
import math

import jax
import jax.numpy as jnp
import numpy as np
from jax import lax
from jax.sharding import Mesh
from jax.sharding import PartitionSpec as P

HD = 128
DP = ("zh", "dl")
HALF = ("dl", "tensor")


def attend_local(query, new_key, new_value, cache_key, cache_value, lengths):
    row_count = query.shape[0]
    cache_len = cache_key.shape[1]
    kv_here = new_key.shape[1] // HD
    grouping = query.shape[1] // (kv_here * HD)
    queries = query.reshape(row_count, kv_here, grouping, HD)
    cache_keys = cache_key.reshape(row_count, cache_len, kv_here, HD)
    values = cache_value.reshape(row_count, cache_len, kv_here, HD)
    own_key = new_key.reshape(row_count, kv_here, HD)
    own_value = new_value.reshape(row_count, kv_here, HD)
    factor = 1.0 / math.sqrt(HD)
    scores = (
        jnp.einsum("rkgd,rckd->rkgc", queries, cache_keys, preferred_element_type=jnp.float32)
        * factor
    )
    own_score = (
        jnp.einsum("rkgd,rkd->rkg", queries, own_key, preferred_element_type=jnp.float32) * factor
    )
    visible = (jnp.arange(cache_len, dtype=jnp.int32)[None, :] < lengths[:, None])[:, None, None, :]
    highest = jnp.maximum(jnp.max(jnp.where(visible, scores, -1e30), axis=-1), own_score)
    exponent = jnp.where(visible, jnp.exp(scores - highest[..., None]), 0.0)
    own_exponent = jnp.exp(own_score - highest)
    totals = jnp.sum(exponent, axis=-1) + own_exponent
    probability = (exponent / totals[..., None]).astype(jnp.bfloat16)
    own_probability = (own_exponent / totals).astype(jnp.bfloat16)
    combined = jnp.einsum(
        "rkgc,rckd->rkgd", probability, values, preferred_element_type=jnp.float32
    )
    combined = (
        combined
        + own_probability.astype(jnp.float32)[..., None]
        * own_value.astype(jnp.float32)[:, :, None, :]
    )
    return combined.reshape(row_count, kv_here * grouping * HD).astype(jnp.bfloat16)


def swap_halves(x):
    return lax.ppermute(x, "zh", [(0, 1), (1, 0)])


def expert_layer(normed, route_ids, route_weight, w_gate, w_up, w_down):
    tok_here, width = normed.shape
    chosen_count = route_ids.shape[1]
    n_half = lax.axis_size("dl") * lax.axis_size("tensor")
    experts_all = 2 * n_half
    capacity = 2 * max(2, 3 * tok_here * chosen_count // experts_all)
    capacity = -(-capacity // 8) * 8
    side = lax.axis_index("zh")
    other_rows = swap_halves(normed)
    packed = swap_halves(jnp.concatenate([route_ids.astype(jnp.float32), route_weight], axis=1))
    other_ids = packed[:, :chosen_count].astype(jnp.int32)
    other_weight = packed[:, chosen_count:]
    rows = jnp.concatenate([normed, other_rows])
    ids = jnp.concatenate([route_ids, other_ids])
    held = 2 * tok_here
    pair_count = held * chosen_count
    local_ids = ids.reshape(pair_count) - side * n_half
    expert_hits = (local_ids[:, None] == jnp.arange(n_half, dtype=jnp.int32)[None, :]).astype(
        jnp.int32
    )
    earlier = jnp.cumsum(expert_hits, axis=0) - expert_hits
    slot_index = jnp.sum(earlier * expert_hits, axis=1)
    in_half = jnp.sum(expert_hits, axis=1) > 0
    target = jnp.where(in_half, local_ids * capacity + slot_index, -1)
    placement = (
        jnp.arange(n_half * capacity, dtype=jnp.int32)[:, None] == target[None, :]
    ).astype(jnp.bfloat16)
    token_place = jnp.sum(placement.reshape(n_half, capacity, held, chosen_count), axis=3)
    own_part = jnp.einsum(
        "hcp,pd->hcd", token_place[:, :, :tok_here], normed, preferred_element_type=jnp.float32
    )
    other_part = jnp.einsum(
        "hcp,pd->hcd", token_place[:, :, tok_here:], other_rows, preferred_element_type=jnp.float32
    )
    outgoing = (own_part + other_part).astype(jnp.bfloat16)
    received = lax.all_to_all(outgoing, HALF, split_axis=0, concat_axis=0, tiled=True)
    gate_part = jnp.einsum("hcd,df->hcf", received, w_gate[0], preferred_element_type=jnp.float32)
    up_part = jnp.einsum("hcd,df->hcf", received, w_up[0], preferred_element_type=jnp.float32)
    activation = (jax.nn.silu(gate_part) * up_part).astype(jnp.bfloat16)
    activation = lax.optimization_barrier(activation)
    result = jnp.einsum(
        "hcf,fd->hcd", activation, w_down[0], preferred_element_type=jnp.float32
    ).astype(jnp.bfloat16)
    lanes = 128
    used = min(capacity, 2 * max(2, 3 * tok_here * chosen_count // experts_all))
    back = result[:, :used].reshape(n_half, used * (width // lanes), lanes)
    returned = lax.all_to_all(back, HALF, split_axis=0, concat_axis=0, tiled=True)
    returned = returned.reshape(n_half * used, width)
    placement = placement.reshape(n_half, capacity, 2, tok_here * chosen_count)[:, :used]
    placement = placement.reshape(n_half * used, 2, tok_here * chosen_count)

    def combine(block, weight):
        pair_rows = jnp.einsum(
            "sp,sd->pd", placement[:, block], returned, preferred_element_type=jnp.float32
        )
        weighted = weight[..., None] * pair_rows.reshape(tok_here, chosen_count, width)
        return jnp.sum(weighted, axis=1)

    sent = swap_halves(combine(1, other_weight).astype(jnp.bfloat16)).astype(jnp.float32)
    return (combine(0, route_weight) + sent).astype(jnp.bfloat16)


def shards(
    query,
    new_key,
    new_value,
    cache_key,
    cache_value,
    lengths,
    hidden_in,
    out_weight,
    norm_gain,
    route_ids,
    route_weight,
    w_gate,
    w_up,
    w_down,
):
    heads_out = attend_local(query, new_key, new_value, cache_key, cache_value, lengths)
    n_dl = lax.axis_size("dl")
    n_t = lax.axis_size("tensor")
    tok_here = hidden_in.shape[0]
    first = lax.axis_index("zh") == 0

    def project(block):
        spread = jnp.broadcast_to(block[None], (n_dl,) + block.shape)
        gathered = lax.all_to_all(spread, "dl", split_axis=0, concat_axis=0, tiled=True)
        return jnp.einsum("sqd,df->sqf", gathered, out_weight, preferred_element_type=jnp.float32)

    own_cols = project(heads_out)
    other_cols = project(swap_halves(heads_out))
    by_side = jnp.where(
        first, jnp.stack([own_cols, other_cols]), jnp.stack([other_cols, own_cols])
    )
    col_width = by_side.shape[-1]
    by_dest = by_side.reshape(2 * n_dl * n_t, tok_here, col_width)
    arrived = lax.all_to_all(
        by_dest.astype(jnp.bfloat16), DP + ("tensor",), split_axis=0, concat_axis=0, tiled=True
    )
    arrived = arrived.astype(jnp.float32).reshape(2 * n_dl, n_t, tok_here, col_width)
    summed = jnp.sum(arrived, axis=1)
    summed = summed.transpose(1, 0, 2).reshape(tok_here, 2 * n_dl * col_width)
    attended = (hidden_in.astype(jnp.float32) + summed).astype(jnp.bfloat16)
    widened = attended.astype(jnp.float32)
    scaled = widened * lax.rsqrt(jnp.mean(widened * widened, axis=-1, keepdims=True) + 1e-06)
    normed = (scaled * norm_gain).astype(jnp.bfloat16)
    expert_mix = expert_layer(normed, route_ids, route_weight, w_gate, w_up, w_down)
    return (attended, expert_mix)


def solution(mesh):
    n_dp = mesh.shape["dp"]
    devices = np.asarray(mesh.devices).reshape(2, n_dp // 2, mesh.shape["tensor"])
    split_mesh = Mesh(devices, ("zh", "dl", "tensor"))
    rows = DP + ("tensor",)
    in_specs = (
        P(DP, "tensor"),
        P(DP, "tensor"),
        P(DP, "tensor"),
        P(DP, None, "tensor"),
        P(DP, None, "tensor"),
        P(DP),
        P(rows, None),
        P("tensor", DP),
        P(),
        P(rows, None),
        P(rows, None),
        P(rows, None, None),
        P(rows, None, None),
        P(rows, None, None),
    )
    out_specs = (P(rows, None), P(rows, None))
    return jax.shard_map(
        shards, mesh=split_mesh, in_specs=in_specs, out_specs=out_specs, check_vma=False
    )
```

```python
import math

import jax
import jax.numpy as jnp
import numpy as np
from jax import lax
from jax.sharding import Mesh
from jax.sharding import PartitionSpec as P

HD = 128
DP = ("zh", "dl")
HALF = ("dl", "tensor")


def attend_local(query, new_key, new_value, cache_key, cache_value, lengths):
    row_count = query.shape[0]
    cache_len = cache_key.shape[1]
    kv_here = new_key.shape[1] // HD
    grouping = query.shape[1] // (kv_here * HD)
    queries = query.reshape(row_count, kv_here, grouping, HD)
    cache_keys = cache_key.reshape(row_count, cache_len, kv_here, HD)
    values = cache_value.reshape(row_count, cache_len, kv_here, HD)
    own_key = new_key.reshape(row_count, kv_here, HD)
    own_value = new_value.reshape(row_count, kv_here, HD)
    factor = 1.0 / math.sqrt(HD)
    scores = (
        jnp.einsum("rkgd,rckd->rkgc", queries, cache_keys, preferred_element_type=jnp.float32)
        * factor
    )
    own_score = (
        jnp.einsum("rkgd,rkd->rkg", queries, own_key, preferred_element_type=jnp.float32) * factor
    )
    visible = (jnp.arange(cache_len, dtype=jnp.int32)[None, :] < lengths[:, None])[:, None, None, :]
    highest = jnp.maximum(jnp.max(jnp.where(visible, scores, -1e30), axis=-1), own_score)
    exponent = jnp.where(visible, jnp.exp(scores - highest[..., None]), 0.0)
    own_exponent = jnp.exp(own_score - highest)
    totals = jnp.sum(exponent, axis=-1) + own_exponent
    probability = (exponent / totals[..., None]).astype(jnp.bfloat16)
    own_probability = (own_exponent / totals).astype(jnp.bfloat16)
    combined = jnp.einsum(
        "rkgc,rckd->rkgd", probability, values, preferred_element_type=jnp.float32
    )
    combined = (
        combined
        + own_probability.astype(jnp.float32)[..., None]
        * own_value.astype(jnp.float32)[:, :, None, :]
    )
    return combined.reshape(row_count, kv_here * grouping * HD).astype(jnp.bfloat16)


def swap_halves(x):
    return lax.ppermute(x, "zh", [(0, 1), (1, 0)])


def expert_layer(normed, route_ids, route_weight, w_gate, w_up, w_down):
    tok_here, width = normed.shape
    chosen_count = route_ids.shape[1]
    n_half = lax.axis_size("dl") * lax.axis_size("tensor")
    experts_all = 2 * n_half
    capacity = 2 * max(2, 3 * tok_here * chosen_count // experts_all)
    capacity = -(-capacity // 8) * 8
    side = lax.axis_index("zh")
    other_rows = swap_halves(normed)
    packed = swap_halves(jnp.concatenate([route_ids.astype(jnp.float32), route_weight], axis=1))
    other_ids = packed[:, :chosen_count].astype(jnp.int32)
    other_weight = packed[:, chosen_count:]
    rows = jnp.concatenate([normed, other_rows])
    ids = jnp.concatenate([route_ids, other_ids])
    held = 2 * tok_here
    pair_count = held * chosen_count
    local_ids = ids.reshape(pair_count) - side * n_half
    expert_hits = (local_ids[:, None] == jnp.arange(n_half, dtype=jnp.int32)[None, :]).astype(
        jnp.int32
    )
    earlier = jnp.cumsum(expert_hits, axis=0) - expert_hits
    slot_index = jnp.sum(earlier * expert_hits, axis=1)
    in_half = jnp.sum(expert_hits, axis=1) > 0
    target = jnp.where(in_half, local_ids * capacity + slot_index, -1)
    placement = (
        jnp.arange(n_half * capacity, dtype=jnp.int32)[:, None] == target[None, :]
    ).astype(jnp.bfloat16)
    token_place = jnp.sum(placement.reshape(n_half, capacity, held, chosen_count), axis=3)
    outgoing = jnp.einsum(
        "hcp,pd->hcd", token_place, rows, preferred_element_type=jnp.float32
    ).astype(jnp.bfloat16)
    received = lax.all_to_all(outgoing, HALF, split_axis=0, concat_axis=0, tiled=True)
    gate_part = jnp.einsum("hcd,df->hcf", received, w_gate[0], preferred_element_type=jnp.float32)
    up_part = jnp.einsum("hcd,df->hcf", received, w_up[0], preferred_element_type=jnp.float32)
    activation = (jax.nn.silu(gate_part) * up_part).astype(jnp.bfloat16)
    activation = lax.optimization_barrier(activation)
    result = jnp.einsum(
        "hcf,fd->hcd", activation, w_down[0], preferred_element_type=jnp.float32
    ).astype(jnp.bfloat16)
    lanes = 128
    used = min(capacity, 2 * max(2, 3 * tok_here * chosen_count // experts_all))
    back = result[:, :used].reshape(n_half, used * (width // lanes), lanes)
    returned = lax.all_to_all(back, HALF, split_axis=0, concat_axis=0, tiled=True)
    returned = returned.reshape(n_half * used, width)
    placement = placement.reshape(n_half, capacity, 2, tok_here * chosen_count)[:, :used]
    placement = placement.reshape(n_half * used, 2, tok_here * chosen_count)

    slot_of = target.reshape(2, tok_here * chosen_count)

    def combine(block, weight):
        slot = slot_of[block]
        slot = jnp.where(slot >= 0, (slot // capacity) * used + slot % capacity, -1)
        picked = jnp.take(returned, jnp.maximum(slot, 0), axis=0)
        pair_rows = jnp.where((slot >= 0)[:, None], picked.astype(jnp.float32), 0.0)
        weighted = weight[..., None] * pair_rows.reshape(tok_here, chosen_count, width)
        return jnp.sum(weighted, axis=1)

    sent = swap_halves(combine(1, other_weight).astype(jnp.bfloat16)).astype(jnp.float32)
    return (combine(0, route_weight) + sent).astype(jnp.bfloat16)


def shards(
    query,
    new_key,
    new_value,
    cache_key,
    cache_value,
    lengths,
    hidden_in,
    out_weight,
    norm_gain,
    route_ids,
    route_weight,
    w_gate,
    w_up,
    w_down,
):
    heads_out = attend_local(query, new_key, new_value, cache_key, cache_value, lengths)
    n_dl = lax.axis_size("dl")
    n_t = lax.axis_size("tensor")
    tok_here = hidden_in.shape[0]
    first = lax.axis_index("zh") == 0

    def project(block):
        spread = jnp.broadcast_to(block[None], (n_dl,) + block.shape)
        gathered = lax.all_to_all(spread, "dl", split_axis=0, concat_axis=0, tiled=True)
        return jnp.einsum("sqd,df->sqf", gathered, out_weight, preferred_element_type=jnp.float32)

    own_cols = project(heads_out)
    other_cols = project(swap_halves(heads_out))
    by_side = jnp.where(
        first, jnp.stack([own_cols, other_cols]), jnp.stack([other_cols, own_cols])
    )
    col_width = by_side.shape[-1]
    by_dest = by_side.reshape(2 * n_dl * n_t, tok_here, col_width)
    arrived = lax.all_to_all(
        by_dest.astype(jnp.bfloat16), DP + ("tensor",), split_axis=0, concat_axis=0, tiled=True
    )
    arrived = arrived.astype(jnp.float32).reshape(2 * n_dl, n_t, tok_here, col_width)
    summed = jnp.sum(arrived, axis=1)
    summed = summed.transpose(1, 0, 2).reshape(tok_here, 2 * n_dl * col_width)
    attended = (hidden_in.astype(jnp.float32) + summed).astype(jnp.bfloat16)
    widened = attended.astype(jnp.float32)
    scaled = widened * lax.rsqrt(jnp.mean(widened * widened, axis=-1, keepdims=True) + 1e-06)
    normed = (scaled * norm_gain).astype(jnp.bfloat16)
    expert_mix = expert_layer(normed, route_ids, route_weight, w_gate, w_up, w_down)
    return (attended, expert_mix)


def solution(mesh):
    n_dp = mesh.shape["dp"]
    devices = np.asarray(mesh.devices).reshape(2, n_dp // 2, mesh.shape["tensor"])
    split_mesh = Mesh(devices, ("zh", "dl", "tensor"))
    rows = DP + ("tensor",)
    in_specs = (
        P(DP, "tensor"),
        P(DP, "tensor"),
        P(DP, "tensor"),
        P(DP, None, "tensor"),
        P(DP, None, "tensor"),
        P(DP),
        P(rows, None),
        P("tensor", DP),
        P(),
        P(rows, None),
        P(rows, None),
        P(rows, None, None),
        P(rows, None, None),
        P(rows, None, None),
    )
    out_specs = (P(rows, None), P(rows, None))
    return jax.shard_map(
        shards, mesh=split_mesh, in_specs=in_specs, out_specs=out_specs, check_vma=False
    )
```
